256 devices in a mesh: seq: 16 (over x, y), head: 16 (over z, core).
Axes of the slice: x: 4, y: 4, z: 8, core: 2. Of those that a mesh axis runs over, the one named last changes fastest.
Arguments:
- queries: bfloat16 [32768, 8192], P(('seq', 'head')), may hold values from -17 to 17
- key_vectors: bfloat16 [32768, 8192], P(('seq', 'head')), may hold values from -6 to 6
- values: bfloat16 [32768, 8192], P(('seq', 'head')), may hold values from -17 to 17
- gate_logits: bfloat16 [32768, 8192], P(('seq', 'head')), may hold values from -6 to 6
- norm_gain: bfloat16 [8192], replicated, may hold values from 0.25 to 1.75
Outputs:
- gated_output: bfloat16 [32768, 8192], P(('seq', 'head'))
The draws below stay inside these ranges and needn't reach their ends.
All inputs are finite; a program needn't handle non-finite values.
Results may differ from the reference program's by a relative error of at most 0.0058.
Values may be sent and summed in bfloat16 or wider, within the bound.
No kernel may reach another device: no remote copies, remote signals or barrier semaphores. Data moves between devices by JAX's collectives and lax.ppermute only.
A program may use at most 64 MiB of HBM per device.

```python
import math
import jax
import jax.numpy as jnp
from jax import lax

H = 64
E = 128
BLK = 512
TOKENS = 32768


def draw_queries(key, part):
    row_key = jax.random.fold_in(key, 11)
    entry_key = jax.random.fold_in(key, 12)
    row_scale = jnp.exp(jax.random.uniform(row_key, (TOKENS, 1), jnp.float32, 0.0, math.log(10.0)))
    normals = jnp.clip(jax.random.normal(entry_key, (TOKENS, H * E), jnp.float32), -5.0, 5.0)
    return (normals * row_scale / 3.0).astype(jnp.bfloat16)


def draw_values(key, part):
    column_key = jax.random.fold_in(key, 21)
    entry_key = jax.random.fold_in(key, 22)
    column_scale = jnp.exp(jax.random.uniform(column_key, (1, H * E), jnp.float32, 0.0, math.log(10.0)))
    normals = jnp.clip(jax.random.normal(entry_key, (TOKENS, H * E), jnp.float32), -5.0, 5.0)
    return (normals * column_scale / 3.0).astype(jnp.bfloat16)


def levels(key, extent, split, least, top_value):
    def one(position, blocks):
        steps = jax.random.uniform(jax.random.fold_in(jax.random.fold_in(key, 6), position), (blocks,), jnp.float32, least / len(split), top_value / len(split))
        return jnp.repeat(jnp.exp(steps), extent[position] // blocks).reshape((-1,) + (1,) * (len(extent) - position - 1))

    gain = one(*split[0])
    for cut in split[1:]:
        gain = gain * one(*cut)
    return gain


def normal_values(own_key, shape, scale, bound, split=(), kind=jnp.bfloat16):
    factor_of = levels(own_key, shape, split, -0.22, 0.18) if split else 1.0
    array = jax.random.normal(own_key, shape, jnp.float32) * scale * factor_of
    return jnp.minimum(jnp.maximum(array, -bound), bound).astype(kind)


def setup_inputs(seed: int = 0) -> dict:
    keys = jax.random.split(jax.random.key(seed), 6)
    return {
        "queries": draw_queries(jax.random.fold_in(keys[5], 71), 0),
        "key_vectors": normal_values(keys[1], (TOKENS, H * E), 1.0, 6.0, ((0, 256),)),
        "values": draw_values(jax.random.fold_in(keys[5], 71), 0),
        "gate_logits": normal_values(keys[3], (TOKENS, H * E), 1.5, 6.0, ((0, 256),)),
        "norm_gain": jnp.clip(1.0 + 0.15 * jax.random.normal(keys[4], (H * E,), jnp.float32), 0.25, 1.75).astype(jnp.bfloat16),
    }


def head_attention(queries, key_vectors, values, head_index):
    offset = head_index * E
    query_cols = lax.dynamic_slice_in_dim(queries, offset, E, 1).astype(jnp.float32).reshape(-1, BLK, E)
    key_cols = lax.dynamic_slice_in_dim(key_vectors, offset, E, 1).astype(jnp.float32).reshape(-1, BLK, E)
    value_cols = lax.dynamic_slice_in_dim(values, offset, E, 1).astype(jnp.float32).reshape(-1, BLK, E)
    block_state = jnp.einsum('nbe,nbf->nef', key_cols, value_cols, precision=lax.Precision.HIGHEST)
    prefix = jnp.concatenate([jnp.zeros_like(block_state[:1]), jnp.cumsum(block_state[:-1], axis=0)], axis=0)
    prefix = lax.optimization_barrier(prefix.astype(jnp.bfloat16)).astype(jnp.float32)
    scores = jnp.einsum('nbe,nce->nbc', query_cols, key_cols, precision=lax.Precision.HIGHEST)
    lower_mask = lax.broadcasted_iota(jnp.int32, (BLK, BLK), 0) >= lax.broadcasted_iota(jnp.int32, (BLK, BLK), 1)
    weights = jnp.where(lower_mask[None], scores, 0.0).astype(jnp.bfloat16)
    weights = lax.optimization_barrier(weights).astype(jnp.float32)
    local_part = jnp.einsum('nbc,nce->nbe', weights, value_cols, precision=lax.Precision.HIGHEST)
    carried_part = jnp.einsum('nbe,nef->nbf', query_cols, prefix, precision=lax.Precision.HIGHEST)
    return (local_part + carried_part).astype(jnp.bfloat16).reshape(-1, E)

def reference(queries, key_vectors, values, gate_logits, norm_gain):

    def one_head(head_index):
        return head_attention(queries, key_vectors, values, head_index)
    stacked = lax.map(one_head, jnp.arange(H, dtype=jnp.int32))
    attended = jnp.transpose(stacked, (1, 0, 2)).reshape(TOKENS, H * E)
    features = attended.astype(jnp.float32)
    mean_square = lax.optimization_barrier(jnp.mean(features * features, axis=1, keepdims=True))
    scaled = features * lax.rsqrt(mean_square + 1e-06) * norm_gain.astype(jnp.float32)[None, :]
    scaled = scaled * jax.nn.sigmoid(gate_logits.astype(jnp.float32))
    return scaled.astype(jnp.bfloat16)
```

```python
import jax
import jax.numpy as jnp
from jax import lax
from jax.sharding import Mesh
from jax.sharding import PartitionSpec as P

E = 128
SWAP = [(0, 1), (1, 0)]


def on_device(queries, key_vectors, values, gate_logits, norm_gain):
    tokens = queries.shape[0]
    heads = queries.shape[1] // E
    chips = lax.axis_size("z")
    core = lax.axis_index("core")
    shard = lax.axis_index("seq")
    query_heads = queries.reshape(tokens, heads, E)
    key_heads = key_vectors.reshape(tokens, heads, E)
    value_heads = values.reshape(tokens, heads, E)

    state = jnp.einsum("the,thf->hef", key_heads, value_heads, preferred_element_type=jnp.float32)

    scores = jnp.einsum("the,she->hts", query_heads, key_heads, preferred_element_type=jnp.float32)
    lower_mask = lax.broadcasted_iota(jnp.int32, (tokens, tokens), 0) >= lax.broadcasted_iota(
        jnp.int32, (tokens, tokens), 1
    )
    weights = jnp.where(lower_mask[None], scores, 0.0).astype(jnp.bfloat16)
    local_part = jnp.einsum("hts,she->the", weights, value_heads, preferred_element_type=jnp.float32)

    other_state = lax.ppermute(state, "core", SWAP)
    chip_state = state + other_state
    half = lax.dynamic_index_in_dim(chip_state.reshape(2, heads // 2, E, E), core, 0, False)
    pieces = half.reshape(chips, heads // 2 // chips, E, E).astype(jnp.bfloat16)
    by_chip = lax.all_to_all(pieces, "z", 0, 0, tiled=True).astype(jnp.float32)

    shard_total = jnp.sum(by_chip, axis=0)
    totals = lax.all_gather(shard_total, "seq")
    earlier = (lax.broadcasted_iota(jnp.int32, (totals.shape[0], 1, 1, 1), 0) < shard).astype(jnp.float32)
    entering = jnp.sum(totals * earlier, axis=0)
    within = jnp.cumsum(by_chip, axis=0) - by_chip
    prefix_pieces = (entering[None] + within).astype(jnp.bfloat16)

    own_half = lax.all_to_all(prefix_pieces, "z", 0, 0, tiled=True).reshape(heads // 2, E, E)
    other_half = lax.ppermute(own_half, "core", SWAP)
    first = core == 0
    prefix = jnp.concatenate(
        [jnp.where(first, own_half, other_half), jnp.where(first, other_half, own_half)], axis=0
    )
    before_me = jnp.where(first, 0.0, other_state).astype(jnp.bfloat16)

    carried_part = jnp.einsum("the,hef->thf", query_heads, prefix, preferred_element_type=jnp.float32)
    carried_part += jnp.einsum("the,hef->thf", query_heads, before_me, preferred_element_type=jnp.float32)
    attended = (local_part + carried_part).astype(jnp.bfloat16).reshape(tokens, heads * E)

    features = attended.astype(jnp.float32)
    mean_square = jnp.mean(features * features, axis=1, keepdims=True)
    scaled = features * lax.rsqrt(mean_square + 1e-06) * norm_gain.astype(jnp.float32)[None, :]
    scaled = scaled * jax.nn.sigmoid(gate_logits.astype(jnp.float32))
    return scaled.astype(jnp.bfloat16)


def solution(mesh):
    seq = mesh.shape["seq"]
    cores = 2
    chips = mesh.shape["head"] // cores
    split = Mesh(mesh.devices.reshape(seq, chips, cores), ("seq", "z", "core"))
    rows = P(("seq", "z", "core"), None)
    return jax.shard_map(
        on_device,
        mesh=split,
        in_specs=(rows, rows, rows, rows, P()),
        out_specs=rows,
        check_vma=False,
    )
```

```python
import jax
import jax.numpy as jnp
from jax import lax
from jax.sharding import PartitionSpec as P

E = 128


def on_device(queries, key_vectors, values, gate_logits, norm_gain):
    tokens = queries.shape[0]
    heads = queries.shape[1] // E
    chips = lax.axis_size("head") // 2
    core = lax.axis_index("head") % 2
    pieces_of = heads // 2 // chips
    pairs = [(h, h ^ 1) for h in range(2 * chips)]
    query_heads = queries.reshape(tokens, heads, E)
    key_heads = key_vectors.reshape(tokens, heads, E)
    value_heads = values.reshape(tokens, heads, E)

    state = jnp.einsum("the,thf->hef", key_heads, value_heads, preferred_element_type=jnp.float32)

    scores = jnp.einsum("the,she->hts", query_heads, key_heads, preferred_element_type=jnp.float32)
    lower_mask = lax.broadcasted_iota(jnp.int32, (tokens, tokens), 0) >= lax.broadcasted_iota(
        jnp.int32, (tokens, tokens), 1
    )
    weights = jnp.where(lower_mask[None], scores, 0.0).astype(jnp.bfloat16)
    local_part = jnp.einsum("hts,she->the", weights, value_heads, preferred_element_type=jnp.float32)

    other_state = lax.ppermute(state, "head", pairs)
    chip_state = (state + other_state).reshape(2, chips, pieces_of, 2, E // 2, E)
    my_rows = lax.dynamic_index_in_dim(chip_state, core, 3, False)
    outgoing = jnp.swapaxes(my_rows, 0, 1).reshape(2 * chips, pieces_of, E // 2, E)
    incoming = lax.all_to_all(outgoing.astype(jnp.bfloat16), "head", 0, 0, tiled=True)
    by_chip = jnp.swapaxes(incoming.reshape(chips, 2, pieces_of, E // 2, E), 1, 2)
    by_chip = by_chip.reshape(chips, pieces_of, E, E).astype(jnp.float32)

    shard_total = jnp.sum(by_chip, axis=0)
    shards = lax.axis_size("seq")
    parts = jnp.swapaxes(shard_total.reshape(pieces_of, shards, E // shards, E), 0, 1)
    per_shard = lax.all_to_all(parts, "seq", 0, 0, tiled=True)
    running = jnp.cumsum(per_shard, axis=0)
    before = jnp.concatenate([jnp.zeros_like(running[:1]), running[:-1]], axis=0)
    entering = lax.all_to_all(before, "seq", 0, 0, tiled=True)
    entering = jnp.swapaxes(entering, 0, 1).reshape(pieces_of, E, E)

    running = jnp.cumsum(by_chip, axis=0)
    within = jnp.concatenate([jnp.zeros_like(running[:1]), running[:-1]], axis=0)
    prefix_pieces = (entering[None] + within).astype(jnp.bfloat16)
    outgoing = jnp.swapaxes(prefix_pieces.reshape(chips, pieces_of, 2, E // 2, E), 1, 2)
    outgoing = outgoing.reshape(2 * chips, pieces_of, E // 2, E)
    returned = lax.all_to_all(outgoing, "head", 0, 0, tiled=True)
    own_rows = jnp.swapaxes(returned.reshape(chips, 2, pieces_of, E // 2, E), 0, 1)
    own_rows = own_rows.reshape(heads, E // 2, E)
    other_rows = lax.ppermute(own_rows, "head", pairs)
    first = core == 0
    prefix = jnp.concatenate(
        [jnp.where(first, own_rows, other_rows), jnp.where(first, other_rows, own_rows)], axis=1
    )
    before_me = jnp.where(first, 0.0, other_state).astype(jnp.bfloat16)

    carried_part = jnp.einsum("the,hef->thf", query_heads, prefix, preferred_element_type=jnp.float32)
    carried_part += jnp.einsum("the,hef->thf", query_heads, before_me, preferred_element_type=jnp.float32)
    attended = (local_part + carried_part).astype(jnp.bfloat16).reshape(tokens, heads * E)

    features = attended.astype(jnp.float32)
    mean_square = jnp.mean(features * features, axis=1, keepdims=True)
    scaled = features * lax.rsqrt(mean_square + 1e-06) * norm_gain.astype(jnp.float32)[None, :]
    scaled = scaled * jax.nn.sigmoid(gate_logits.astype(jnp.float32))
    return scaled.astype(jnp.bfloat16)


def solution(mesh):
    rows = P(("seq", "head"), None)
    return jax.shard_map(
        on_device,
        mesh=mesh,
        in_specs=(rows, rows, rows, rows, P()),
        out_specs=rows,
        check_vma=False,
    )
```

```python
import jax
import jax.numpy as jnp
from jax import lax
from jax.experimental import pallas as pl
from jax.experimental.pallas import tpu as pltpu
from jax.sharding import PartitionSpec as P

E = 128
GROUP = 8


def state_kernel(key_ref, value_ref, state_ref):
    for j in range(GROUP):
        cols = slice(j * E, (j + 1) * E)
        state_ref[j] = lax.dot_general(
            key_ref[:, cols], value_ref[:, cols], (((0,), (0,)), ((), ())),
            preferred_element_type=jnp.float32,
        )


def block_states(key_vectors, values):
    tokens, width = key_vectors.shape
    heads = width // E
    cols = pl.BlockSpec((tokens, GROUP * E), lambda i: (0, i))
    return pl.pallas_call(
        state_kernel,
        grid=(heads // GROUP,),
        in_specs=[cols, cols],
        out_specs=pl.BlockSpec((GROUP, E, E), lambda i: (i, 0, 0)),
        out_shape=jax.ShapeDtypeStruct((heads, E, E), jnp.float32),
    )(key_vectors, values)


def output_kernel(query_ref, key_ref, value_ref, prefix_ref, before_ref, gate_ref, gain_ref,
                  out_ref, attended_ref, square_ref):
    step = pl.program_id(0)
    tokens = query_ref.shape[0]

    @pl.when(step == 0)
    def _():
        square_ref[...] = jnp.zeros_like(square_ref)

    lower_mask = lax.broadcasted_iota(jnp.int32, (tokens, tokens), 0) >= lax.broadcasted_iota(
        jnp.int32, (tokens, tokens), 1
    )
    for j in range(GROUP):
        cols = slice(j * E, (j + 1) * E)
        query = query_ref[:, cols]
        value = value_ref[:, cols]
        scores = lax.dot_general(
            query, key_ref[:, cols], (((1,), (1,)), ((), ())), preferred_element_type=jnp.float32
        )
        weights = jnp.where(lower_mask, scores, 0.0).astype(jnp.bfloat16)
        total = jnp.dot(weights, value, preferred_element_type=jnp.float32)
        total += jnp.dot(query, prefix_ref[j], preferred_element_type=jnp.float32)
        total += jnp.dot(query, before_ref[j], preferred_element_type=jnp.float32)
        attended = total.astype(jnp.bfloat16)
        start = pl.multiple_of((step * GROUP + j) * E, E)
        attended_ref[:, pl.ds(start, E)] = attended
        features = attended.astype(jnp.float32)
        square_ref[...] += features * features

    @pl.when(step == pl.num_programs(0) - 1)
    def _():
        width = attended_ref.shape[1]
        mean_square = jnp.sum(square_ref[...], axis=1, keepdims=True) / width
        scale = lax.rsqrt(mean_square + 1e-06)

        def chunk(c, carry):
            start = pl.multiple_of(c * E, E)
            window = pl.ds(start, E)
            features = attended_ref[:, window].astype(jnp.float32)
            gain = gain_ref[:, window].astype(jnp.float32)
            gate = gate_ref[:, window].astype(jnp.float32)
            scaled = features * scale * gain
            scaled = scaled * (1.0 / (1.0 + jnp.exp(-gate)))
            out_ref[:, window] = scaled.astype(out_ref.dtype)
            return carry

        lax.fori_loop(0, width // E, chunk, 0)


def gated_attention(queries, key_vectors, values, prefix, before, gate_logits, norm_gain):
    tokens, width = queries.shape
    heads = width // E
    cols = pl.BlockSpec((tokens, GROUP * E), lambda i: (0, i))
    states = pl.BlockSpec((GROUP, E, E), lambda i: (i, 0, 0))
    whole = pl.BlockSpec((tokens, width), lambda i: (0, 0))
    return pl.pallas_call(
        output_kernel,
        grid=(heads // GROUP,),
        in_specs=[cols, cols, cols, states, states, whole, pl.BlockSpec((1, width), lambda i: (0, 0))],
        out_specs=whole,
        out_shape=jax.ShapeDtypeStruct((tokens, width), jnp.bfloat16),
        scratch_shapes=[pltpu.VMEM((tokens, width), jnp.bfloat16), pltpu.VMEM((tokens, E), jnp.float32)],
    )(queries, key_vectors, values, prefix, before, gate_logits, norm_gain.reshape(1, width))


def on_device(queries, key_vectors, values, gate_logits, norm_gain):
    heads = queries.shape[1] // E
    chips = lax.axis_size("head") // 2
    core = lax.axis_index("head") % 2
    pieces_of = heads // 2 // chips
    pairs = [(h, h ^ 1) for h in range(2 * chips)]

    state = block_states(key_vectors, values)

    other_state = lax.ppermute(state, "head", pairs)
    layout = (2, chips, pieces_of, 2, E // 2, E)
    my_rows = lax.dynamic_index_in_dim(state.reshape(layout), core, 3, False) + lax.dynamic_index_in_dim(
        other_state.reshape(layout), core, 3, False
    )
    outgoing = jnp.swapaxes(my_rows, 0, 1).reshape(2 * chips, pieces_of, E // 2, E)
    incoming = lax.all_to_all(outgoing.astype(jnp.bfloat16), "head", 0, 0, tiled=True)
    by_chip = jnp.swapaxes(incoming.reshape(chips, 2, pieces_of, E // 2, E), 1, 2)
    by_chip = by_chip.reshape(chips, pieces_of, E, E).astype(jnp.float32)

    shard_total = jnp.sum(by_chip, axis=0)
    shards = lax.axis_size("seq")
    parts = jnp.swapaxes(shard_total.reshape(pieces_of, shards, E // shards, E), 0, 1)
    per_shard = lax.all_to_all(parts, "seq", 0, 0, tiled=True)
    running = jnp.cumsum(per_shard, axis=0)
    before = jnp.concatenate([jnp.zeros_like(running[:1]), running[:-1]], axis=0)
    entering = lax.all_to_all(before, "seq", 0, 0, tiled=True)
    entering = jnp.swapaxes(entering, 0, 1).reshape(pieces_of, E, E)

    running = jnp.cumsum(by_chip, axis=0)
    within = jnp.concatenate([jnp.zeros_like(running[:1]), running[:-1]], axis=0)
    prefix_pieces = (entering[None] + within).astype(jnp.bfloat16)
    outgoing = jnp.swapaxes(prefix_pieces.reshape(chips, pieces_of, 2, E // 2, E), 1, 2)
    outgoing = outgoing.reshape(2 * chips, pieces_of, E // 2, E)
    returned = lax.all_to_all(outgoing, "head", 0, 0, tiled=True)
    own_rows = jnp.swapaxes(returned.reshape(chips, 2, pieces_of, E // 2, E), 0, 1)
    own_rows = own_rows.reshape(heads, E // 2, E)
    other_rows = lax.ppermute(own_rows, "head", pairs)
    first = core == 0
    prefix = jnp.concatenate(
        [jnp.where(first, own_rows, other_rows), jnp.where(first, other_rows, own_rows)], axis=1
    )
    before_me = jnp.where(first, 0.0, other_state).astype(jnp.bfloat16)

    return gated_attention(queries, key_vectors, values, prefix, before_me, gate_logits, norm_gain)


def solution(mesh):
    rows = P(("seq", "head"), None)
    return jax.shard_map(
        on_device,
        mesh=mesh,
        in_specs=(rows, rows, rows, rows, P()),
        out_specs=rows,
        check_vma=False,
    )
```

```python
import jax
import jax.numpy as jnp
from jax import lax
from jax.experimental import pallas as pl
from jax.experimental.pallas import tpu as pltpu
from jax.sharding import PartitionSpec as P

E = 128
GROUP = 8


def state_kernel(key_ref, value_ref, state_ref):
    for j in range(GROUP):
        cols = slice(j * E, (j + 1) * E)
        state_ref[j] = lax.dot_general(
            key_ref[:, cols], value_ref[:, cols], (((0,), (0,)), ((), ())),
            preferred_element_type=jnp.float32,
        )


def block_states(key_vectors, values):
    tokens, width = key_vectors.shape
    heads = width // E
    cols = pl.BlockSpec((tokens, GROUP * E), lambda i: (0, i))
    return pl.pallas_call(
        state_kernel,
        grid=(heads // GROUP,),
        in_specs=[cols, cols],
        out_specs=pl.BlockSpec((GROUP, E, E), lambda i: (i, 0, 0)),
        out_shape=jax.ShapeDtypeStruct((heads, E, E), jnp.float32),
    )(key_vectors, values)


def output_kernel(query_ref, key_ref, value_ref, prefix_ref, before_ref, gate_ref, gain_ref,
                  out_ref, attended_ref, square_ref):
    step = pl.program_id(0)
    tokens = query_ref.shape[0]

    @pl.when(step == 0)
    def _():
        square_ref[...] = jnp.zeros_like(square_ref)

    lower_mask = lax.broadcasted_iota(jnp.int32, (tokens, tokens), 0) >= lax.broadcasted_iota(
        jnp.int32, (tokens, tokens), 1
    )
    for j in range(GROUP):
        cols = slice(j * E, (j + 1) * E)
        query = query_ref[:, cols]
        value = value_ref[:, cols]
        scores = lax.dot_general(
            query, key_ref[:, cols], (((1,), (1,)), ((), ())), preferred_element_type=jnp.float32
        )
        weights = jnp.where(lower_mask, scores, 0.0).astype(jnp.bfloat16)
        total = jnp.dot(weights, value, preferred_element_type=jnp.float32)
        total += jnp.dot(query, prefix_ref[j], preferred_element_type=jnp.float32)
        total += jnp.dot(query, before_ref[j], preferred_element_type=jnp.float32)
        attended = total.astype(jnp.bfloat16)
        start = pl.multiple_of((step * GROUP + j) * E, E)
        attended_ref[:, pl.ds(start, E)] = attended
        features = attended.astype(jnp.float32)
        square_ref[...] += features * features

    @pl.when(step == pl.num_programs(0) - 1)
    def _():
        width = attended_ref.shape[1]
        mean_square = jnp.sum(square_ref[...], axis=1, keepdims=True) / width
        scale = lax.rsqrt(mean_square + 1e-06)

        def chunk(c, carry):
            start = pl.multiple_of(c * E, E)
            window = pl.ds(start, E)
            features = attended_ref[:, window].astype(jnp.float32)
            gain = gain_ref[:, window].astype(jnp.float32)
            gate = gate_ref[:, window].astype(jnp.float32)
            scaled = features * scale * gain
            scaled = scaled * (1.0 / (1.0 + jnp.exp(-gate)))
            out_ref[:, window] = scaled.astype(out_ref.dtype)
            return carry

        lax.fori_loop(0, width // E, chunk, 0)


def gated_attention(queries, key_vectors, values, prefix, before, gate_logits, norm_gain):
    tokens, width = queries.shape
    heads = width // E
    cols = pl.BlockSpec((tokens, GROUP * E), lambda i: (0, i))
    states = pl.BlockSpec((GROUP, E, E), lambda i: (i, 0, 0))
    whole = pl.BlockSpec((tokens, width), lambda i: (0, 0))
    return pl.pallas_call(
        output_kernel,
        grid=(heads // GROUP,),
        in_specs=[cols, cols, cols, states, states, whole, pl.BlockSpec((1, width), lambda i: (0, 0))],
        out_specs=whole,
        out_shape=jax.ShapeDtypeStruct((tokens, width), jnp.bfloat16),
        scratch_shapes=[pltpu.VMEM((tokens, width), jnp.bfloat16), pltpu.VMEM((tokens, E), jnp.float32)],
    )(queries, key_vectors, values, prefix, before, gate_logits, norm_gain.reshape(1, width))


def exchange(pieces, axis):
    count = pieces.shape[0]
    me = lax.axis_index(axis)
    arrived = [lax.dynamic_index_in_dim(pieces, me, 0, True)]
    for shift in range(1, count):
        piece = lax.dynamic_index_in_dim(pieces, (me + shift) % count, 0, True)
        arrived.append(lax.ppermute(piece, axis, [(i, (i + shift) % count) for i in range(count)]))
    return jnp.roll(jnp.concatenate(arrived[::-1], axis=0), me + 1, axis=0)


def on_device(queries, key_vectors, values, gate_logits, norm_gain):
    heads = queries.shape[1] // E
    chips = lax.axis_size("head") // 2
    core = lax.axis_index("head") % 2
    pieces_of = heads // 2 // chips
    pairs = [(h, h ^ 1) for h in range(2 * chips)]

    state = block_states(key_vectors, values)

    other_state = lax.ppermute(state, "head", pairs)
    layout = (2, chips, pieces_of, 2, E // 2, E)
    my_rows = lax.dynamic_index_in_dim(state.reshape(layout), core, 3, False) + lax.dynamic_index_in_dim(
        other_state.reshape(layout), core, 3, False
    )
    outgoing = jnp.swapaxes(my_rows, 0, 1).reshape(2 * chips, pieces_of, E // 2, E)
    incoming = exchange(outgoing.astype(jnp.bfloat16), "head")
    by_chip = jnp.swapaxes(incoming.reshape(chips, 2, pieces_of, E // 2, E), 1, 2)
    by_chip = by_chip.reshape(chips, pieces_of, E, E).astype(jnp.float32)

    shard_total = jnp.sum(by_chip, axis=0)
    shards = lax.axis_size("seq")
    parts = jnp.swapaxes(shard_total.reshape(pieces_of, shards, E // shards, E), 0, 1)
    per_shard = lax.all_to_all(parts, "seq", 0, 0, tiled=True)
    running = jnp.cumsum(per_shard, axis=0)
    before = jnp.concatenate([jnp.zeros_like(running[:1]), running[:-1]], axis=0)
    entering = lax.all_to_all(before, "seq", 0, 0, tiled=True)
    entering = jnp.swapaxes(entering, 0, 1).reshape(pieces_of, E, E)

    running = jnp.cumsum(by_chip, axis=0)
    within = jnp.concatenate([jnp.zeros_like(running[:1]), running[:-1]], axis=0)
    prefix_pieces = (entering[None] + within).astype(jnp.bfloat16)
    outgoing = jnp.swapaxes(prefix_pieces.reshape(chips, pieces_of, 2, E // 2, E), 1, 2)
    outgoing = outgoing.reshape(2 * chips, pieces_of, E // 2, E)
    returned = exchange(outgoing, "head")
    own_rows = jnp.swapaxes(returned.reshape(chips, 2, pieces_of, E // 2, E), 0, 1)
    own_rows = own_rows.reshape(heads, E // 2, E)
    other_rows = lax.ppermute(own_rows, "head", pairs)
    first = core == 0
    prefix = jnp.concatenate(
        [jnp.where(first, own_rows, other_rows), jnp.where(first, other_rows, own_rows)], axis=1
    )
    before_me = jnp.where(first, 0.0, other_state).astype(jnp.bfloat16)

    return gated_attention(queries, key_vectors, values, prefix, before_me, gate_logits, norm_gain)


def solution(mesh):
    rows = P(("seq", "head"), None)
    return jax.shard_map(
        on_device,
        mesh=mesh,
        in_specs=(rows, rows, rows, rows, P()),
        out_specs=rows,
        check_vma=False,
    )
```

```python
import jax
import jax.numpy as jnp
from jax import lax
from jax.experimental import pallas as pl
from jax.experimental.pallas import tpu as pltpu
from jax.sharding import PartitionSpec as P

E = 128
GROUP = 8


def state_kernel(key_ref, value_ref, state_ref):
    for j in range(GROUP):
        cols = slice(j * E, (j + 1) * E)
        state_ref[j] = lax.dot_general(
            key_ref[:, cols], value_ref[:, cols], (((0,), (0,)), ((), ())),
            preferred_element_type=jnp.float32,
        )


def block_states(key_vectors, values):
    tokens, width = key_vectors.shape
    heads = width // E
    cols = pl.BlockSpec((tokens, GROUP * E), lambda i: (0, i))
    return pl.pallas_call(
        state_kernel,
        grid=(heads // GROUP,),
        in_specs=[cols, cols],
        out_specs=pl.BlockSpec((GROUP, E, E), lambda i: (i, 0, 0)),
        out_shape=jax.ShapeDtypeStruct((heads, E, E), jnp.float32),
    )(key_vectors, values)


def output_kernel(query_ref, key_ref, value_ref, prefix_ref, before_ref, gate_ref, gain_ref,
                  out_ref, attended_ref, square_ref):
    step = pl.program_id(0)
    tokens = query_ref.shape[0]

    @pl.when(step == 0)
    def _():
        square_ref[...] = jnp.zeros_like(square_ref)

    lower_mask = lax.broadcasted_iota(jnp.int32, (tokens, tokens), 0) >= lax.broadcasted_iota(
        jnp.int32, (tokens, tokens), 1
    )
    for j in range(GROUP):
        cols = slice(j * E, (j + 1) * E)
        query = query_ref[:, cols]
        value = value_ref[:, cols]
        scores = lax.dot_general(
            query, key_ref[:, cols], (((1,), (1,)), ((), ())), preferred_element_type=jnp.float32
        )
        weights = jnp.where(lower_mask, scores, 0.0).astype(jnp.bfloat16)
        total = jnp.dot(weights, value, preferred_element_type=jnp.float32)
        total += jnp.dot(query, prefix_ref[j], preferred_element_type=jnp.float32)
        total += jnp.dot(query, before_ref[j], preferred_element_type=jnp.float32)
        attended = total.astype(jnp.bfloat16)
        start = pl.multiple_of((step * GROUP + j) * E, E)
        attended_ref[:, pl.ds(start, E)] = attended
        features = attended.astype(jnp.float32)
        square_ref[...] += features * features

    @pl.when(step == pl.num_programs(0) - 1)
    def _():
        width = attended_ref.shape[1]
        mean_square = jnp.sum(square_ref[...], axis=1, keepdims=True) / width
        scale = lax.rsqrt(mean_square + 1e-06)

        def chunk(c, carry):
            start = pl.multiple_of(c * E, E)
            window = pl.ds(start, E)
            features = attended_ref[:, window].astype(jnp.float32)
            gain = gain_ref[:, window].astype(jnp.float32)
            gate = gate_ref[:, window].astype(jnp.float32)
            scaled = features * scale * gain
            scaled = scaled * (1.0 / (1.0 + jnp.exp(-gate)))
            out_ref[:, window] = scaled.astype(out_ref.dtype)
            return carry

        lax.fori_loop(0, width // E, chunk, 0)


def gated_attention(queries, key_vectors, values, prefix, before, gate_logits, norm_gain):
    tokens, width = queries.shape
    heads = width // E
    cols = pl.BlockSpec((tokens, GROUP * E), lambda i: (0, i))
    states = pl.BlockSpec((GROUP, E, E), lambda i: (i, 0, 0))
    whole = pl.BlockSpec((tokens, width), lambda i: (0, 0))
    return pl.pallas_call(
        output_kernel,
        grid=(heads // GROUP,),
        in_specs=[cols, cols, cols, states, states, whole, pl.BlockSpec((1, width), lambda i: (0, 0))],
        out_specs=whole,
        out_shape=jax.ShapeDtypeStruct((tokens, width), jnp.bfloat16),
        scratch_shapes=[pltpu.VMEM((tokens, width), jnp.bfloat16), pltpu.VMEM((tokens, E), jnp.float32)],
    )(queries, key_vectors, values, prefix, before, gate_logits, norm_gain.reshape(1, width))


def on_device(queries, key_vectors, values, gate_logits, norm_gain):
    heads = queries.shape[1] // E
    chips = lax.axis_size("head") // 2
    core = lax.axis_index("head") % 2
    pieces_of = heads // 2 // chips
    pairs = [(h, h ^ 1) for h in range(2 * chips)]

    state = block_states(key_vectors, values)

    other_state = lax.ppermute(state, "head", pairs)
    layout = (2, chips, pieces_of, 2, E // 2, E)
    my_rows = lax.dynamic_index_in_dim(state.reshape(layout), core, 3, False) + lax.dynamic_index_in_dim(
        other_state.reshape(layout), core, 3, False
    )
    shards = lax.axis_size("seq")
    rows_of = E // 2 // shards
    outgoing = my_rows.reshape(2, chips, pieces_of, shards, rows_of, E).transpose(3, 1, 0, 2, 4, 5)
    outgoing = outgoing.reshape(shards * 2 * chips, pieces_of, rows_of, E).astype(jnp.bfloat16)
    incoming = lax.all_to_all(outgoing, ("seq", "head"), 0, 0, tiled=True)
    by_chip = incoming.reshape(shards * chips, 2, pieces_of, rows_of, E).astype(jnp.float32)

    running = jnp.cumsum(by_chip, axis=0)
    before = jnp.concatenate([jnp.zeros_like(running[:1]), running[:-1]], axis=0).astype(jnp.bfloat16)
    returned = lax.all_to_all(
        before.reshape(shards * chips * 2, pieces_of, rows_of, E), ("seq", "head"), 0, 0, tiled=True
    )
    own_rows = returned.reshape(shards, chips, 2, pieces_of, rows_of, E).transpose(2, 1, 3, 0, 4, 5)
    own_rows = own_rows.reshape(heads, E // 2, E)
    other_rows = lax.ppermute(own_rows, "head", pairs)
    first = core == 0
    prefix = jnp.concatenate(
        [jnp.where(first, own_rows, other_rows), jnp.where(first, other_rows, own_rows)], axis=1
    )
    before_me = jnp.where(first, 0.0, other_state).astype(jnp.bfloat16)

    return gated_attention(queries, key_vectors, values, prefix, before_me, gate_logits, norm_gain)


def solution(mesh):
    rows = P(("seq", "head"), None)
    return jax.shard_map(
        on_device,
        mesh=mesh,
        in_specs=(rows, rows, rows, rows, P()),
        out_specs=rows,
        check_vma=False,
    )
```

```python
import jax
import jax.numpy as jnp
from jax import lax
from jax.experimental import pallas as pl
from jax.experimental.pallas import tpu as pltpu
from jax.sharding import PartitionSpec as P

E = 128
GROUP = 16


def state_kernel(key_ref, value_ref, state_ref):
    for j in range(GROUP):
        cols = slice(j * E, (j + 1) * E)
        state_ref[j] = lax.dot_general(
            key_ref[:, cols], value_ref[:, cols], (((0,), (0,)), ((), ())),
            preferred_element_type=jnp.float32,
        )


def block_states(key_vectors, values):
    tokens, width = key_vectors.shape
    heads = width // E
    cols = pl.BlockSpec((tokens, GROUP * E), lambda i: (0, i))
    return pl.pallas_call(
        state_kernel,
        grid=(heads // GROUP,),
        in_specs=[cols, cols],
        out_specs=pl.BlockSpec((GROUP, E, E), lambda i: (i, 0, 0)),
        out_shape=jax.ShapeDtypeStruct((heads, E, E), jnp.float32),
    )(key_vectors, values)


def output_kernel(query_ref, key_ref, value_ref, prefix_ref, before_ref, gate_ref, gain_ref,
                  out_ref, attended_ref, square_ref):
    step = pl.program_id(0)
    tokens = query_ref.shape[0]

    @pl.when(step == 0)
    def _():
        square_ref[...] = jnp.zeros_like(square_ref)

    lower_mask = lax.broadcasted_iota(jnp.int32, (tokens, tokens), 0) >= lax.broadcasted_iota(
        jnp.int32, (tokens, tokens), 1
    )
    for j in range(GROUP):
        cols = slice(j * E, (j + 1) * E)
        query = query_ref[:, cols]
        value = value_ref[:, cols]
        scores = lax.dot_general(
            query, key_ref[:, cols], (((1,), (1,)), ((), ())), preferred_element_type=jnp.float32
        )
        weights = jnp.where(lower_mask, scores, 0.0).astype(jnp.bfloat16)
        total = jnp.dot(weights, value, preferred_element_type=jnp.float32)
        total += jnp.dot(query, prefix_ref[j], preferred_element_type=jnp.float32)
        total += jnp.dot(query, before_ref[j], preferred_element_type=jnp.float32)
        attended = total.astype(jnp.bfloat16)
        start = pl.multiple_of((step * GROUP + j) * E, E)
        attended_ref[:, pl.ds(start, E)] = attended
        features = attended.astype(jnp.float32)
        square_ref[...] += features * features

    @pl.when(step == pl.num_programs(0) - 1)
    def _():
        width = attended_ref.shape[1]
        mean_square = jnp.sum(square_ref[...], axis=1, keepdims=True) / width
        scale = lax.rsqrt(mean_square + 1e-06)

        def chunk(c, carry):
            start = pl.multiple_of(c * E, E)
            window = pl.ds(start, E)
            features = attended_ref[:, window].astype(jnp.float32)
            gain = gain_ref[:, window].astype(jnp.float32)
            gate = gate_ref[:, window].astype(jnp.float32)
            scaled = features * scale * gain
            scaled = scaled * (1.0 / (1.0 + jnp.exp(-gate)))
            out_ref[:, window] = scaled.astype(out_ref.dtype)
            return carry

        lax.fori_loop(0, width // E, chunk, 0)


def gated_attention(queries, key_vectors, values, prefix, before, gate_logits, norm_gain):
    tokens, width = queries.shape
    heads = width // E
    cols = pl.BlockSpec((tokens, GROUP * E), lambda i: (0, i))
    states = pl.BlockSpec((GROUP, E, E), lambda i: (i, 0, 0))
    whole = pl.BlockSpec((tokens, width), lambda i: (0, 0))
    return pl.pallas_call(
        output_kernel,
        grid=(heads // GROUP,),
        in_specs=[cols, cols, cols, states, states, whole, pl.BlockSpec((1, width), lambda i: (0, 0))],
        out_specs=whole,
        out_shape=jax.ShapeDtypeStruct((tokens, width), jnp.bfloat16),
        scratch_shapes=[pltpu.VMEM((tokens, width), jnp.bfloat16), pltpu.VMEM((tokens, E), jnp.float32)],
    )(queries, key_vectors, values, prefix, before, gate_logits, norm_gain.reshape(1, width))


def on_device(queries, key_vectors, values, gate_logits, norm_gain):
    heads = queries.shape[1] // E
    chips = lax.axis_size("head") // 2
    core = lax.axis_index("head") % 2
    pieces_of = heads // 2 // chips
    pairs = [(h, h ^ 1) for h in range(2 * chips)]

    state = block_states(key_vectors, values)

    halves = state.reshape(heads, 2, E // 2, E)
    partner_half = lax.ppermute(lax.dynamic_index_in_dim(halves, 1 - core, 1, False), "head", pairs)
    my_rows = lax.dynamic_index_in_dim(halves, core, 1, False) + partner_half
    first_half = lax.ppermute(halves[:, 0].astype(jnp.bfloat16), "head", [(h, h + 1) for h in range(0, 2 * chips, 2)])
    shards = lax.axis_size("seq")
    rows_of = E // 2 // shards
    outgoing = my_rows.reshape(2, chips, pieces_of, shards, rows_of, E).transpose(3, 1, 0, 2, 4, 5)
    outgoing = outgoing.reshape(shards * 2 * chips, pieces_of, rows_of, E).astype(jnp.bfloat16)
    incoming = lax.all_to_all(outgoing, ("seq", "head"), 0, 0, tiled=True)
    by_chip = incoming.reshape(shards * chips, 2, pieces_of, rows_of, E).astype(jnp.float32)

    running = jnp.cumsum(by_chip, axis=0)
    before = jnp.concatenate([jnp.zeros_like(running[:1]), running[:-1]], axis=0).astype(jnp.bfloat16)
    returned = lax.all_to_all(
        before.reshape(shards * chips * 2, pieces_of, rows_of, E), ("seq", "head"), 0, 0, tiled=True
    )
    own_rows = returned.reshape(shards, chips, 2, pieces_of, rows_of, E).transpose(2, 1, 3, 0, 4, 5)
    own_rows = own_rows.reshape(heads, E // 2, E)
    other_rows = lax.ppermute(own_rows, "head", pairs)
    first = core == 0
    prefix = jnp.concatenate(
        [jnp.where(first, own_rows, other_rows), jnp.where(first, other_rows, own_rows)], axis=1
    )
    before_me = jnp.concatenate(
        [jnp.where(first, 0.0, first_half), jnp.where(first, 0.0, partner_half).astype(jnp.bfloat16)], axis=1
    ).astype(jnp.bfloat16)

    return gated_attention(queries, key_vectors, values, prefix, before_me, gate_logits, norm_gain)


def solution(mesh):
    rows = P(("seq", "head"), None)
    return jax.shard_map(
        on_device,
        mesh=mesh,
        in_specs=(rows, rows, rows, rows, P()),
        out_specs=rows,
        check_vma=False,
    )
```

```python
import jax
import jax.numpy as jnp
from jax import lax
from jax.experimental import pallas as pl
from jax.experimental.pallas import tpu as pltpu
from jax.sharding import PartitionSpec as P

E = 128
GROUP = 16


def state_kernel(key_ref, value_ref, state_ref):
    for j in range(GROUP):
        cols = slice(j * E, (j + 1) * E)
        state_ref[j] = lax.dot_general(
            key_ref[:, cols], value_ref[:, cols], (((0,), (0,)), ((), ())),
            preferred_element_type=jnp.float32,
        )


def block_states(key_vectors, values):
    tokens, width = key_vectors.shape
    heads = width // E
    cols = pl.BlockSpec((tokens, GROUP * E), lambda i: (0, i))
    return pl.pallas_call(
        state_kernel,
        grid=(heads // GROUP,),
        in_specs=[cols, cols],
        out_specs=pl.BlockSpec((GROUP, E, E), lambda i: (i, 0, 0)),
        out_shape=jax.ShapeDtypeStruct((heads, E, E), jnp.float32),
    )(key_vectors, values)


def output_kernel(core_ref, query_ref, key_ref, value_ref, own_ref, other_ref, first_ref, partner_ref,
                  gate_ref, gain_ref, out_ref, attended_ref, square_ref):
    step = pl.program_id(0)
    tokens = query_ref.shape[0]
    first = core_ref[0] == 0

    @pl.when(step == 0)
    def _():
        square_ref[...] = jnp.zeros_like(square_ref)

    lower_mask = lax.broadcasted_iota(jnp.int32, (tokens, tokens), 0) >= lax.broadcasted_iota(
        jnp.int32, (tokens, tokens), 1
    )
    for j in range(GROUP):
        cols = slice(j * E, (j + 1) * E)
        query = query_ref[:, cols]
        value = value_ref[:, cols]
        scores = lax.dot_general(
            query, key_ref[:, cols], (((1,), (1,)), ((), ())), preferred_element_type=jnp.float32
        )
        weights = jnp.where(lower_mask, scores, 0.0).astype(jnp.bfloat16)
        total = jnp.dot(weights, value, preferred_element_type=jnp.float32)
        own = own_ref[j]
        other = other_ref[j]
        prefix = jnp.concatenate([jnp.where(first, own, other), jnp.where(first, other, own)], axis=0)
        total += jnp.dot(query, prefix, preferred_element_type=jnp.float32)
        before = jnp.concatenate([first_ref[j], partner_ref[j].astype(jnp.bfloat16)], axis=0)
        before_part = jnp.dot(query, before, preferred_element_type=jnp.float32)
        total += jnp.where(first, 0.0, before_part)
        attended = total.astype(jnp.bfloat16)
        start = pl.multiple_of((step * GROUP + j) * E, E)
        attended_ref[:, pl.ds(start, E)] = attended
        features = attended.astype(jnp.float32)
        square_ref[...] += features * features

    @pl.when(step == pl.num_programs(0) - 1)
    def _():
        width = attended_ref.shape[1]
        mean_square = jnp.sum(square_ref[...], axis=1, keepdims=True) / width
        scale = lax.rsqrt(mean_square + 1e-06)

        def chunk(c, carry):
            start = pl.multiple_of(c * E, E)
            window = pl.ds(start, E)
            features = attended_ref[:, window].astype(jnp.float32)
            gain = gain_ref[:, window].astype(jnp.float32)
            gate = gate_ref[:, window].astype(jnp.float32)
            scaled = features * scale * gain
            scaled = scaled * (1.0 / (1.0 + jnp.exp(-gate)))
            out_ref[:, window] = scaled.astype(out_ref.dtype)
            return carry

        lax.fori_loop(0, width // E, chunk, 0)


def gated_attention(core, queries, key_vectors, values, own, other, first_half, partner_half,
                    gate_logits, norm_gain):
    tokens, width = queries.shape
    heads = width // E
    cols = pl.BlockSpec((tokens, GROUP * E), lambda i, core: (0, i))
    halves = pl.BlockSpec((GROUP, E // 2, E), lambda i, core: (i, 0, 0))
    whole = pl.BlockSpec((tokens, width), lambda i, core: (0, 0))
    return pl.pallas_call(
        output_kernel,
        grid_spec=pltpu.PrefetchScalarGridSpec(
            num_scalar_prefetch=1,
            grid=(heads // GROUP,),
            in_specs=[cols, cols, cols, halves, halves, halves, halves, whole,
                      pl.BlockSpec((1, width), lambda i, core: (0, 0))],
            out_specs=whole,
            scratch_shapes=[pltpu.VMEM((tokens, width), jnp.bfloat16), pltpu.VMEM((tokens, E), jnp.float32)],
        ),
        out_shape=jax.ShapeDtypeStruct((tokens, width), jnp.bfloat16),
    )(core.reshape(1), queries, key_vectors, values, own, other, first_half, partner_half, gate_logits,
      norm_gain.reshape(1, width))


def on_device(queries, key_vectors, values, gate_logits, norm_gain):
    heads = queries.shape[1] // E
    chips = lax.axis_size("head") // 2
    core = lax.axis_index("head") % 2
    pieces_of = heads // 2 // chips
    pairs = [(h, h ^ 1) for h in range(2 * chips)]

    state = block_states(key_vectors, values)

    halves = state.reshape(heads, 2, E // 2, E)
    partner_half = lax.ppermute(lax.dynamic_index_in_dim(halves, 1 - core, 1, False), "head", pairs)
    my_rows = lax.dynamic_index_in_dim(halves, core, 1, False) + partner_half
    first_half = lax.ppermute(halves[:, 0].astype(jnp.bfloat16), "head", [(h, h + 1) for h in range(0, 2 * chips, 2)])
    devices = lax.axis_size("seq") * 2 * chips
    outgoing = my_rows.astype(jnp.bfloat16).reshape(devices, -1, E)
    incoming = lax.all_to_all(outgoing, ("seq", "head"), 0, 0, tiled=True)
    by_chip = incoming.reshape(devices // 2, 2, -1, E).astype(jnp.float32)

    running = jnp.cumsum(by_chip, axis=0)
    before = jnp.concatenate([jnp.zeros_like(running[:1]), running[:-1]], axis=0).astype(jnp.bfloat16)
    returned = lax.all_to_all(before.reshape(devices, -1, E), ("seq", "head"), 0, 0, tiled=True)
    own_rows = returned.reshape(heads, E // 2, E)
    other_rows = lax.ppermute(own_rows, "head", pairs)
    return gated_attention(core, queries, key_vectors, values, own_rows, other_rows, first_half, partner_half,
                           gate_logits, norm_gain)


def solution(mesh):
    rows = P(("seq", "head"), None)
    return jax.shard_map(
        on_device,
        mesh=mesh,
        in_specs=(rows, rows, rows, rows, P()),
        out_specs=rows,
        check_vma=False,
    )
```

```python
import jax
import jax.numpy as jnp
from jax import lax
from jax.experimental import pallas as pl
from jax.experimental.pallas import tpu as pltpu
from jax.sharding import PartitionSpec as P

E = 128
GROUP = 16


def state_kernel(core_ref, key_ref, value_ref, mine_ref, partner_ref, first_ref):
    first = core_ref[0] == 0
    half = E // 2
    for j in range(GROUP):
        cols = slice(j * E, (j + 1) * E)
        state = lax.dot_general(
            key_ref[:, cols], value_ref[:, cols], (((0,), (0,)), ((), ())),
            preferred_element_type=jnp.float32,
        )
        upper, lower = state[:half], state[half:]
        mine_ref[j] = jnp.where(first, upper, lower)
        partner_ref[j] = jnp.where(first, lower, upper)
        first_ref[j] = upper.astype(jnp.bfloat16)


def block_states(core, key_vectors, values):
    tokens, width = key_vectors.shape
    heads = width // E
    cols = pl.BlockSpec((tokens, GROUP * E), lambda i, core: (0, i))
    halves = pl.BlockSpec((GROUP, E // 2, E), lambda i, core: (i, 0, 0))
    shape = (heads, E // 2, E)
    return pl.pallas_call(
        state_kernel,
        grid_spec=pltpu.PrefetchScalarGridSpec(
            num_scalar_prefetch=1, grid=(heads // GROUP,), in_specs=[cols, cols], out_specs=[halves] * 3
        ),
        out_shape=[jax.ShapeDtypeStruct(shape, jnp.float32), jax.ShapeDtypeStruct(shape, jnp.float32),
                   jax.ShapeDtypeStruct(shape, jnp.bfloat16)],
    )(core.reshape(1), key_vectors, values)


def near_kernel(core_ref, query_ref, key_ref, value_ref, first_ref, partner_ref, near_ref):
    tokens = query_ref.shape[0]
    first = core_ref[0] == 0
    lower_mask = lax.broadcasted_iota(jnp.int32, (tokens, tokens), 0) >= lax.broadcasted_iota(
        jnp.int32, (tokens, tokens), 1
    )
    for j in range(GROUP):
        cols = slice(j * E, (j + 1) * E)
        query = query_ref[:, cols]
        scores = lax.dot_general(
            query, key_ref[:, cols], (((1,), (1,)), ((), ())), preferred_element_type=jnp.float32
        )
        weights = jnp.where(lower_mask, scores, 0.0).astype(jnp.bfloat16)
        total = jnp.dot(weights, value_ref[:, cols], preferred_element_type=jnp.float32)
        before = jnp.concatenate([first_ref[j], partner_ref[j].astype(jnp.bfloat16)], axis=0)
        before_part = jnp.dot(query, before, preferred_element_type=jnp.float32)
        near_ref[:, cols] = total + jnp.where(first, 0.0, before_part)


def near_attention(core, queries, key_vectors, values, first_half, partner_half):
    tokens, width = queries.shape
    heads = width // E
    cols = pl.BlockSpec((tokens, GROUP * E), lambda i, core: (0, i))
    halves = pl.BlockSpec((GROUP, E // 2, E), lambda i, core: (i, 0, 0))
    return pl.pallas_call(
        near_kernel,
        grid_spec=pltpu.PrefetchScalarGridSpec(
            num_scalar_prefetch=1, grid=(heads // GROUP,), in_specs=[cols, cols, cols, halves, halves],
            out_specs=cols,
        ),
        out_shape=jax.ShapeDtypeStruct((tokens, width), jnp.float32),
    )(core.reshape(1), queries, key_vectors, values, first_half, partner_half)


def output_kernel(core_ref, query_ref, near_ref, own_ref, other_ref, gate_ref, gain_ref,
                  out_ref, attended_ref, square_ref):
    step = pl.program_id(0)
    first = core_ref[0] == 0

    @pl.when(step == 0)
    def _():
        square_ref[...] = jnp.zeros_like(square_ref)

    for j in range(GROUP):
        cols = slice(j * E, (j + 1) * E)
        own = own_ref[j]
        other = other_ref[j]
        prefix = jnp.concatenate([jnp.where(first, own, other), jnp.where(first, other, own)], axis=0)
        total = near_ref[:, cols] + jnp.dot(query_ref[:, cols], prefix, preferred_element_type=jnp.float32)
        attended = total.astype(jnp.bfloat16)
        start = pl.multiple_of((step * GROUP + j) * E, E)
        attended_ref[:, pl.ds(start, E)] = attended
        features = attended.astype(jnp.float32)
        square_ref[...] += features * features

    @pl.when(step == pl.num_programs(0) - 1)
    def _():
        width = attended_ref.shape[1]
        mean_square = jnp.sum(square_ref[...], axis=1, keepdims=True) / width
        scale = lax.rsqrt(mean_square + 1e-06)

        def chunk(c, carry):
            start = pl.multiple_of(c * E, E)
            window = pl.ds(start, E)
            features = attended_ref[:, window].astype(jnp.float32)
            gain = gain_ref[:, window].astype(jnp.float32)
            gate = gate_ref[:, window].astype(jnp.float32)
            scaled = features * scale * gain
            scaled = scaled * (1.0 / (1.0 + jnp.exp(-gate)))
            out_ref[:, window] = scaled.astype(out_ref.dtype)
            return carry

        lax.fori_loop(0, width // E, chunk, 0)


def gated_attention(core, queries, near, own, other, gate_logits, norm_gain):
    tokens, width = queries.shape
    heads = width // E
    cols = pl.BlockSpec((tokens, GROUP * E), lambda i, core: (0, i))
    halves = pl.BlockSpec((GROUP, E // 2, E), lambda i, core: (i, 0, 0))
    whole = pl.BlockSpec((tokens, width), lambda i, core: (0, 0))
    return pl.pallas_call(
        output_kernel,
        grid_spec=pltpu.PrefetchScalarGridSpec(
            num_scalar_prefetch=1,
            grid=(heads // GROUP,),
            in_specs=[cols, pl.BlockSpec((tokens, GROUP * E), lambda i, core: (0, i)), halves, halves, whole,
                      pl.BlockSpec((1, width), lambda i, core: (0, 0))],
            out_specs=whole,
            scratch_shapes=[pltpu.VMEM((tokens, width), jnp.bfloat16), pltpu.VMEM((tokens, E), jnp.float32)],
        ),
        out_shape=jax.ShapeDtypeStruct((tokens, width), jnp.bfloat16),
    )(core.reshape(1), queries, near, own, other, gate_logits,
      norm_gain.reshape(1, width))


def on_device(queries, key_vectors, values, gate_logits, norm_gain):
    heads = queries.shape[1] // E
    chips = lax.axis_size("head") // 2
    core = lax.axis_index("head") % 2
    pairs = [(h, h ^ 1) for h in range(2 * chips)]

    mine, for_partner, first_rows = block_states(core, key_vectors, values)
    partner_half = lax.ppermute(for_partner, "head", pairs)
    my_rows = mine + partner_half
    first_half = lax.ppermute(first_rows, "head", [(h, h + 1) for h in range(0, 2 * chips, 2)])
    devices = lax.axis_size("seq") * 2 * chips
    outgoing = my_rows.astype(jnp.bfloat16).reshape(devices, -1, E)
    incoming = lax.all_to_all(outgoing, ("seq", "head"), 0, 0, tiled=True)
    by_chip = incoming.reshape(devices // 2, 2, -1, E).astype(jnp.float32)

    running = jnp.cumsum(by_chip, axis=0)
    before = jnp.concatenate([jnp.zeros_like(running[:1]), running[:-1]], axis=0).astype(jnp.bfloat16)
    returned = lax.all_to_all(before.reshape(devices, -1, E), ("seq", "head"), 0, 0, tiled=True)
    near = near_attention(core, queries, key_vectors, values, first_half, partner_half)
    own_rows = returned.reshape(heads, E // 2, E)
    other_rows = lax.ppermute(own_rows, "head", pairs)
    return gated_attention(core, queries, near, own_rows, other_rows, gate_logits, norm_gain)


def solution(mesh):
    rows = P(("seq", "head"), None)
    return jax.shard_map(
        on_device,
        mesh=mesh,
        in_specs=(rows, rows, rows, rows, P()),
        out_specs=rows,
        check_vma=False,
    )
```

```python
import jax
import jax.numpy as jnp
from jax import lax
from jax.experimental import pallas as pl
from jax.experimental.pallas import tpu as pltpu
from jax.sharding import PartitionSpec as P

E = 128
GROUP = 16


def state_kernel(core_ref, key_ref, value_ref, mine_ref, partner_ref, first_ref):
    first = core_ref[0] == 0
    half = E // 2
    for j in range(GROUP):
        cols = slice(j * E, (j + 1) * E)
        state = lax.dot_general(
            key_ref[:, cols], value_ref[:, cols], (((0,), (0,)), ((), ())),
            preferred_element_type=jnp.float32,
        )
        upper, lower = state[:half], state[half:]
        mine_ref[j] = jnp.where(first, upper, lower)
        partner_ref[j] = jnp.where(first, lower, upper)
        first_ref[j] = upper.astype(jnp.bfloat16)


def block_states(core, key_vectors, values):
    tokens, width = key_vectors.shape
    heads = width // E
    cols = pl.BlockSpec((tokens, GROUP * E), lambda i, core: (0, i))
    halves = pl.BlockSpec((GROUP, E // 2, E), lambda i, core: (i, 0, 0))
    shape = (heads, E // 2, E)
    return pl.pallas_call(
        state_kernel,
        grid_spec=pltpu.PrefetchScalarGridSpec(
            num_scalar_prefetch=1, grid=(heads // GROUP,), in_specs=[cols, cols], out_specs=[halves] * 3
        ),
        out_shape=[jax.ShapeDtypeStruct(shape, jnp.float32), jax.ShapeDtypeStruct(shape, jnp.float32),
                   jax.ShapeDtypeStruct(shape, jnp.bfloat16)],
    )(core.reshape(1), key_vectors, values)


def near_kernel(core_ref, query_ref, key_ref, value_ref, first_ref, partner_ref, mine_ref, near_ref, chip_ref):
    tokens = query_ref.shape[0]
    first = core_ref[0] == 0
    lower_mask = lax.broadcasted_iota(jnp.int32, (tokens, tokens), 0) >= lax.broadcasted_iota(
        jnp.int32, (tokens, tokens), 1
    )
    for j in range(GROUP):
        cols = slice(j * E, (j + 1) * E)
        query = query_ref[:, cols]
        scores = lax.dot_general(
            query, key_ref[:, cols], (((1,), (1,)), ((), ())), preferred_element_type=jnp.float32
        )
        weights = jnp.where(lower_mask, scores, 0.0).astype(jnp.bfloat16)
        total = jnp.dot(weights, value_ref[:, cols], preferred_element_type=jnp.float32)
        before = jnp.concatenate([first_ref[j], partner_ref[j].astype(jnp.bfloat16)], axis=0)
        before_part = jnp.dot(query, before, preferred_element_type=jnp.float32)
        near_ref[:, cols] = total + jnp.where(first, 0.0, before_part)
        chip_ref[j] = (mine_ref[j] + partner_ref[j]).astype(jnp.bfloat16)


def near_attention(core, queries, key_vectors, values, first_half, partner_half, mine):
    tokens, width = queries.shape
    heads = width // E
    cols = pl.BlockSpec((tokens, GROUP * E), lambda i, core: (0, i))
    halves = pl.BlockSpec((GROUP, E // 2, E), lambda i, core: (i, 0, 0))
    return pl.pallas_call(
        near_kernel,
        grid_spec=pltpu.PrefetchScalarGridSpec(
            num_scalar_prefetch=1, grid=(heads // GROUP,), in_specs=[cols, cols, cols, halves, halves, halves],
            out_specs=[cols, halves],
        ),
        out_shape=[jax.ShapeDtypeStruct((tokens, width), jnp.float32),
                   jax.ShapeDtypeStruct((heads, E // 2, E), jnp.bfloat16)],
    )(core.reshape(1), queries, key_vectors, values, first_half, partner_half, mine)


def output_kernel(core_ref, query_ref, near_ref, own_ref, other_ref, gate_ref, gain_ref,
                  out_ref, attended_ref, square_ref, opening_ref):
    step = pl.program_id(0)
    first = core_ref[0] == 0

    @pl.when(step == 0)
    def _():
        square_ref[...] = jnp.zeros_like(square_ref)

    for j in range(GROUP):
        cols = slice(j * E, (j + 1) * E)
        own = own_ref[j]
        other = other_ref[j]
        prefix = jnp.concatenate([jnp.where(first, own, other), jnp.where(first, other, own)], axis=0)
        total = near_ref[:, cols] + jnp.dot(query_ref[:, cols], prefix, preferred_element_type=jnp.float32)
        attended = total.astype(jnp.bfloat16)
        start = pl.multiple_of((step * GROUP + j) * E, E)
        attended_ref[:, pl.ds(start, E)] = attended
        features = attended.astype(jnp.float32)
        square_ref[...] += features * features
        gate = gate_ref[:, cols].astype(jnp.float32)
        opening_ref[:, pl.ds(start, E)] = 1.0 / (1.0 + jnp.exp(-gate))

    @pl.when(step == pl.num_programs(0) - 1)
    def _():
        width = attended_ref.shape[1]
        mean_square = jnp.sum(square_ref[...], axis=1, keepdims=True) / width
        scale = lax.rsqrt(mean_square + 1e-06)

        def chunk(c, carry):
            start = pl.multiple_of(c * E, E)
            window = pl.ds(start, E)
            features = attended_ref[:, window].astype(jnp.float32)
            gain = gain_ref[:, window].astype(jnp.float32)
            scaled = features * scale * gain
            scaled = scaled * opening_ref[:, window]
            out_ref[:, window] = scaled.astype(out_ref.dtype)
            return carry

        lax.fori_loop(0, width // E, chunk, 0)


def gated_attention(core, queries, near, own, other, gate_logits, norm_gain):
    tokens, width = queries.shape
    heads = width // E
    cols = pl.BlockSpec((tokens, GROUP * E), lambda i, core: (0, i))
    halves = pl.BlockSpec((GROUP, E // 2, E), lambda i, core: (i, 0, 0))
    whole = pl.BlockSpec((tokens, width), lambda i, core: (0, 0))
    return pl.pallas_call(
        output_kernel,
        grid_spec=pltpu.PrefetchScalarGridSpec(
            num_scalar_prefetch=1,
            grid=(heads // GROUP,),
            in_specs=[cols, cols, halves, halves, cols,
                      pl.BlockSpec((1, width), lambda i, core: (0, 0))],
            out_specs=whole,
            scratch_shapes=[pltpu.VMEM((tokens, width), jnp.bfloat16), pltpu.VMEM((tokens, E), jnp.float32),
                            pltpu.VMEM((tokens, width), jnp.float32)],
        ),
        out_shape=jax.ShapeDtypeStruct((tokens, width), jnp.bfloat16),
    )(core.reshape(1), queries, near, own, other, gate_logits,
      norm_gain.reshape(1, width))


def on_device(queries, key_vectors, values, gate_logits, norm_gain):
    heads = queries.shape[1] // E
    chips = lax.axis_size("head") // 2
    core = lax.axis_index("head") % 2
    pairs = [(h, h ^ 1) for h in range(2 * chips)]

    mine, for_partner, first_rows = block_states(core, key_vectors, values)
    partner_half = lax.ppermute(for_partner, "head", pairs)
    first_half = lax.ppermute(first_rows, "head", [(h, h + 1) for h in range(0, 2 * chips, 2)])
    near, my_rows = near_attention(core, queries, key_vectors, values, first_half, partner_half, mine)
    devices = lax.axis_size("seq") * 2 * chips
    outgoing = my_rows.reshape(devices, -1, E)
    incoming = lax.all_to_all(outgoing, ("seq", "head"), 0, 0, tiled=True)
    by_chip = incoming.reshape(devices // 2, 2, -1, E).astype(jnp.float32)

    running = jnp.cumsum(by_chip, axis=0)
    before = jnp.concatenate([jnp.zeros_like(running[:1]), running[:-1]], axis=0).astype(jnp.bfloat16)
    returned = lax.all_to_all(before.reshape(devices, -1, E), ("seq", "head"), 0, 0, tiled=True)
    own_rows = returned.reshape(heads, E // 2, E)
    other_rows = lax.ppermute(own_rows, "head", pairs)
    return gated_attention(core, queries, near, own_rows, other_rows, gate_logits, norm_gain)


def solution(mesh):
    rows = P(("seq", "head"), None)
    return jax.shard_map(
        on_device,
        mesh=mesh,
        in_specs=(rows, rows, rows, rows, P()),
        out_specs=rows,
        check_vma=False,
    )
```

```python
import jax
import jax.numpy as jnp
from jax import lax
from jax.experimental import pallas as pl
from jax.experimental.pallas import tpu as pltpu
from jax.sharding import PartitionSpec as P

E = 128
GROUP = 32


def state_kernel(core_ref, key_ref, value_ref, mine_ref, partner_ref, first_ref):
    first = core_ref[0] == 0
    half = E // 2
    for j in range(GROUP):
        cols = slice(j * E, (j + 1) * E)
        state = lax.dot_general(
            key_ref[:, cols], value_ref[:, cols], (((0,), (0,)), ((), ())),
            preferred_element_type=jnp.float32,
        )
        upper, lower = state[:half], state[half:]
        mine_ref[j] = jnp.where(first, upper, lower)
        partner_ref[j] = jnp.where(first, lower, upper)
        first_ref[j] = upper.astype(jnp.bfloat16)


def block_states(core, key_vectors, values):
    tokens, width = key_vectors.shape
    heads = width // E
    cols = pl.BlockSpec((tokens, GROUP * E), lambda i, core: (0, i))
    halves = pl.BlockSpec((GROUP, E // 2, E), lambda i, core: (i, 0, 0))
    shape = (heads, E // 2, E)
    return pl.pallas_call(
        state_kernel,
        grid_spec=pltpu.PrefetchScalarGridSpec(
            num_scalar_prefetch=1, grid=(heads // GROUP,), in_specs=[cols, cols], out_specs=[halves] * 3
        ),
        out_shape=[jax.ShapeDtypeStruct(shape, jnp.float32), jax.ShapeDtypeStruct(shape, jnp.float32),
                   jax.ShapeDtypeStruct(shape, jnp.bfloat16)],
    )(core.reshape(1), key_vectors, values)


def near_kernel(core_ref, query_ref, key_ref, value_ref, first_ref, partner_ref, mine_ref, near_ref, chip_ref):
    tokens = query_ref.shape[0]
    first = core_ref[0] == 0
    lower_mask = lax.broadcasted_iota(jnp.int32, (tokens, tokens), 0) >= lax.broadcasted_iota(
        jnp.int32, (tokens, tokens), 1
    )
    for j in range(GROUP):
        cols = slice(j * E, (j + 1) * E)
        query = query_ref[:, cols]
        scores = lax.dot_general(
            query, key_ref[:, cols], (((1,), (1,)), ((), ())), preferred_element_type=jnp.float32
        )
        weights = jnp.where(lower_mask, scores, 0.0).astype(jnp.bfloat16)
        total = jnp.dot(weights, value_ref[:, cols], preferred_element_type=jnp.float32)
        before = jnp.concatenate([first_ref[j], partner_ref[j].astype(jnp.bfloat16)], axis=0)
        before_part = jnp.dot(query, before, preferred_element_type=jnp.float32)
        near_ref[:, cols] = total + jnp.where(first, 0.0, before_part)
        chip_ref[j] = (mine_ref[j] + partner_ref[j]).astype(jnp.bfloat16)


def near_attention(core, queries, key_vectors, values, first_half, partner_half, mine):
    tokens, width = queries.shape
    heads = width // E
    cols = pl.BlockSpec((tokens, GROUP * E), lambda i, core: (0, i))
    halves = pl.BlockSpec((GROUP, E // 2, E), lambda i, core: (i, 0, 0))
    return pl.pallas_call(
        near_kernel,
        grid_spec=pltpu.PrefetchScalarGridSpec(
            num_scalar_prefetch=1, grid=(heads // GROUP,), in_specs=[cols, cols, cols, halves, halves, halves],
            out_specs=[cols, halves],
        ),
        out_shape=[jax.ShapeDtypeStruct((tokens, width), jnp.float32),
                   jax.ShapeDtypeStruct((heads, E // 2, E), jnp.bfloat16)],
    )(core.reshape(1), queries, key_vectors, values, first_half, partner_half, mine)


def output_kernel(core_ref, query_ref, near_ref, own_ref, other_ref, gate_ref, gain_ref,
                  out_ref, attended_ref, square_ref, opening_ref):
    step = pl.program_id(0)
    first = core_ref[0] == 0

    @pl.when(step == 0)
    def _():
        square_ref[...] = jnp.zeros_like(square_ref)

    for j in range(GROUP):
        cols = slice(j * E, (j + 1) * E)
        own = own_ref[j]
        other = other_ref[j]
        prefix = jnp.concatenate([jnp.where(first, own, other), jnp.where(first, other, own)], axis=0)
        total = near_ref[:, cols] + jnp.dot(query_ref[:, cols], prefix, preferred_element_type=jnp.float32)
        attended = total.astype(jnp.bfloat16)
        start = pl.multiple_of((step * GROUP + j) * E, E)
        attended_ref[:, pl.ds(start, E)] = attended
        features = attended.astype(jnp.float32)
        square_ref[...] += features * features
        gate = gate_ref[:, cols].astype(jnp.float32)
        opening_ref[:, pl.ds(start, E)] = 1.0 / (1.0 + jnp.exp(-gate))

    @pl.when(step == pl.num_programs(0) - 1)
    def _():
        width = attended_ref.shape[1]
        mean_square = jnp.sum(square_ref[...], axis=1, keepdims=True) / width
        scale = lax.rsqrt(mean_square + 1e-06)

        def chunk(c, carry):
            start = pl.multiple_of(c * E, E)
            window = pl.ds(start, E)
            features = attended_ref[:, window].astype(jnp.float32)
            gain = gain_ref[:, window].astype(jnp.float32)
            scaled = features * scale * gain
            scaled = scaled * opening_ref[:, window]
            out_ref[:, window] = scaled.astype(out_ref.dtype)
            return carry

        lax.fori_loop(0, width // E, chunk, 0)


def gated_attention(core, queries, near, own, other, gate_logits, norm_gain):
    tokens, width = queries.shape
    heads = width // E
    cols = pl.BlockSpec((tokens, GROUP * E), lambda i, core: (0, i))
    halves = pl.BlockSpec((GROUP, E // 2, E), lambda i, core: (i, 0, 0))
    whole = pl.BlockSpec((tokens, width), lambda i, core: (0, 0))
    return pl.pallas_call(
        output_kernel,
        grid_spec=pltpu.PrefetchScalarGridSpec(
            num_scalar_prefetch=1,
            grid=(heads // GROUP,),
            in_specs=[cols, cols, halves, halves, cols,
                      pl.BlockSpec((1, width), lambda i, core: (0, 0))],
            out_specs=whole,
            scratch_shapes=[pltpu.VMEM((tokens, width), jnp.bfloat16), pltpu.VMEM((tokens, E), jnp.float32),
                            pltpu.VMEM((tokens, width), jnp.float32)],
        ),
        out_shape=jax.ShapeDtypeStruct((tokens, width), jnp.bfloat16),
    )(core.reshape(1), queries, near, own, other, gate_logits,
      norm_gain.reshape(1, width))


def on_device(queries, key_vectors, values, gate_logits, norm_gain):
    heads = queries.shape[1] // E
    chips = lax.axis_size("head") // 2
    core = lax.axis_index("head") % 2
    pairs = [(h, h ^ 1) for h in range(2 * chips)]

    mine, for_partner, first_rows = block_states(core, key_vectors, values)
    partner_half = lax.ppermute(for_partner, "head", pairs)
    first_half = lax.ppermute(first_rows, "head", [(h, h + 1) for h in range(0, 2 * chips, 2)])
    near, my_rows = near_attention(core, queries, key_vectors, values, first_half, partner_half, mine)
    devices = lax.axis_size("seq") * 2 * chips
    outgoing = my_rows.reshape(devices, -1, E)
    incoming = lax.all_to_all(outgoing, ("seq", "head"), 0, 0, tiled=True)
    by_chip = incoming.reshape(devices // 2, 2, -1, E).astype(jnp.float32)

    running = jnp.cumsum(by_chip, axis=0)
    before = jnp.concatenate([jnp.zeros_like(running[:1]), running[:-1]], axis=0).astype(jnp.bfloat16)
    returned = lax.all_to_all(before.reshape(devices, -1, E), ("seq", "head"), 0, 0, tiled=True)
    own_rows = returned.reshape(heads, E // 2, E)
    other_rows = lax.ppermute(own_rows, "head", pairs)
    return gated_attention(core, queries, near, own_rows, other_rows, gate_logits, norm_gain)


def solution(mesh):
    rows = P(("seq", "head"), None)
    return jax.shard_map(
        on_device,
        mesh=mesh,
        in_specs=(rows, rows, rows, rows, P()),
        out_specs=rows,
        check_vma=False,
    )
```

```python
import jax
import jax.numpy as jnp
from jax import lax
from jax.experimental import pallas as pl
from jax.experimental.pallas import tpu as pltpu
from jax.sharding import PartitionSpec as P

E = 128
GROUP = 32


def state_kernel(core_ref, key_ref, value_ref, mine_ref, partner_ref, first_ref):
    first = core_ref[0] == 0
    half = E // 2
    for j in range(GROUP):
        cols = slice(j * E, (j + 1) * E)
        state = lax.dot_general(
            key_ref[:, cols], value_ref[:, cols], (((0,), (0,)), ((), ())),
            preferred_element_type=jnp.float32,
        )
        upper, lower = state[:half], state[half:]
        mine_ref[j] = jnp.where(first, upper, lower)
        partner_ref[j] = jnp.where(first, lower, upper)
        first_ref[j] = upper.astype(jnp.bfloat16)


def block_states(core, key_vectors, values):
    tokens, width = key_vectors.shape
    heads = width // E
    cols = pl.BlockSpec((tokens, GROUP * E), lambda i, core: (0, i))
    halves = pl.BlockSpec((GROUP, E // 2, E), lambda i, core: (i, 0, 0))
    shape = (heads, E // 2, E)
    return pl.pallas_call(
        state_kernel,
        grid_spec=pltpu.PrefetchScalarGridSpec(
            num_scalar_prefetch=1, grid=(heads // GROUP,), in_specs=[cols, cols], out_specs=[halves] * 3
        ),
        out_shape=[jax.ShapeDtypeStruct(shape, jnp.float32), jax.ShapeDtypeStruct(shape, jnp.float32),
                   jax.ShapeDtypeStruct(shape, jnp.bfloat16)],
    )(core.reshape(1), key_vectors, values)


def local_kernel(query_ref, key_ref, value_ref, local_ref):
    tokens = query_ref.shape[0]
    lower_mask = lax.broadcasted_iota(jnp.int32, (tokens, tokens), 0) >= lax.broadcasted_iota(
        jnp.int32, (tokens, tokens), 1
    )
    for j in range(GROUP):
        cols = slice(j * E, (j + 1) * E)
        scores = lax.dot_general(
            query_ref[:, cols], key_ref[:, cols], (((1,), (1,)), ((), ())),
            preferred_element_type=jnp.float32,
        )
        weights = jnp.where(lower_mask, scores, 0.0).astype(jnp.bfloat16)
        local_ref[:, cols] = jnp.dot(weights, value_ref[:, cols], preferred_element_type=jnp.float32)


def local_attention(queries, key_vectors, values):
    tokens, width = queries.shape
    cols = pl.BlockSpec((tokens, GROUP * E), lambda i: (0, i))
    return pl.pallas_call(
        local_kernel,
        grid=(width // E // GROUP,),
        in_specs=[cols, cols, cols],
        out_specs=cols,
        out_shape=jax.ShapeDtypeStruct((tokens, width), jnp.float32),
    )(queries, key_vectors, values)


def near_kernel(core_ref, query_ref, local_ref, first_ref, partner_ref, mine_ref, near_ref, chip_ref):
    first = core_ref[0] == 0
    for j in range(GROUP):
        cols = slice(j * E, (j + 1) * E)
        partner = partner_ref[j]
        before = jnp.concatenate([first_ref[j], partner.astype(jnp.bfloat16)], axis=0)
        before_part = jnp.dot(query_ref[:, cols], before, preferred_element_type=jnp.float32)
        near_ref[:, cols] = local_ref[:, cols] + jnp.where(first, 0.0, before_part)
        chip_ref[j] = (mine_ref[j] + partner).astype(jnp.bfloat16)


def near_attention(core, queries, local, first_half, partner_half, mine):
    tokens, width = queries.shape
    heads = width // E
    cols = pl.BlockSpec((tokens, GROUP * E), lambda i, core: (0, i))
    halves = pl.BlockSpec((GROUP, E // 2, E), lambda i, core: (i, 0, 0))
    return pl.pallas_call(
        near_kernel,
        grid_spec=pltpu.PrefetchScalarGridSpec(
            num_scalar_prefetch=1, grid=(heads // GROUP,), in_specs=[cols, cols, halves, halves, halves],
            out_specs=[cols, halves],
        ),
        out_shape=[jax.ShapeDtypeStruct((tokens, width), jnp.float32),
                   jax.ShapeDtypeStruct((heads, E // 2, E), jnp.bfloat16)],
    )(core.reshape(1), queries, local, first_half, partner_half, mine)


def output_kernel(core_ref, query_ref, near_ref, own_ref, other_ref, gate_ref, gain_ref,
                  out_ref, attended_ref, square_ref, opening_ref):
    step = pl.program_id(0)
    first = core_ref[0] == 0

    @pl.when(step == 0)
    def _():
        square_ref[...] = jnp.zeros_like(square_ref)

    for j in range(GROUP):
        cols = slice(j * E, (j + 1) * E)
        own = own_ref[j]
        other = other_ref[j]
        prefix = jnp.concatenate([jnp.where(first, own, other), jnp.where(first, other, own)], axis=0)
        total = near_ref[:, cols] + jnp.dot(query_ref[:, cols], prefix, preferred_element_type=jnp.float32)
        attended = total.astype(jnp.bfloat16)
        start = pl.multiple_of((step * GROUP + j) * E, E)
        attended_ref[:, pl.ds(start, E)] = attended
        features = attended.astype(jnp.float32)
        square_ref[...] += features * features
        gate = gate_ref[:, cols].astype(jnp.float32)
        opening_ref[:, pl.ds(start, E)] = 1.0 / (1.0 + jnp.exp(-gate))

    @pl.when(step == pl.num_programs(0) - 1)
    def _():
        width = attended_ref.shape[1]
        mean_square = jnp.sum(square_ref[...], axis=1, keepdims=True) / width
        scale = lax.rsqrt(mean_square + 1e-06)

        def chunk(c, carry):
            start = pl.multiple_of(c * E, E)
            window = pl.ds(start, E)
            features = attended_ref[:, window].astype(jnp.float32)
            gain = gain_ref[:, window].astype(jnp.float32)
            scaled = features * scale * gain
            scaled = scaled * opening_ref[:, window]
            out_ref[:, window] = scaled.astype(out_ref.dtype)
            return carry

        lax.fori_loop(0, width // E, chunk, 0)


def gated_attention(core, queries, near, own, other, gate_logits, norm_gain):
    tokens, width = queries.shape
    heads = width // E
    cols = pl.BlockSpec((tokens, GROUP * E), lambda i, core: (0, i))
    halves = pl.BlockSpec((GROUP, E // 2, E), lambda i, core: (i, 0, 0))
    whole = pl.BlockSpec((tokens, width), lambda i, core: (0, 0))
    return pl.pallas_call(
        output_kernel,
        grid_spec=pltpu.PrefetchScalarGridSpec(
            num_scalar_prefetch=1,
            grid=(heads // GROUP,),
            in_specs=[cols, cols, halves, halves, cols,
                      pl.BlockSpec((1, width), lambda i, core: (0, 0))],
            out_specs=whole,
            scratch_shapes=[pltpu.VMEM((tokens, width), jnp.bfloat16), pltpu.VMEM((tokens, E), jnp.float32),
                            pltpu.VMEM((tokens, width), jnp.float32)],
        ),
        out_shape=jax.ShapeDtypeStruct((tokens, width), jnp.bfloat16),
    )(core.reshape(1), queries, near, own, other, gate_logits,
      norm_gain.reshape(1, width))


def on_device(queries, key_vectors, values, gate_logits, norm_gain):
    heads = queries.shape[1] // E
    chips = lax.axis_size("head") // 2
    core = lax.axis_index("head") % 2
    pairs = [(h, h ^ 1) for h in range(2 * chips)]

    mine, for_partner, first_rows = block_states(core, key_vectors, values)
    partner_half = lax.ppermute(for_partner, "head", pairs)
    first_half = lax.ppermute(first_rows, "head", [(h, h + 1) for h in range(0, 2 * chips, 2)])
    local = local_attention(queries, key_vectors, values)
    near, my_rows = near_attention(core, queries, local, first_half, partner_half, mine)
    devices = lax.axis_size("seq") * 2 * chips
    outgoing = my_rows.reshape(devices, -1, E)
    incoming = lax.all_to_all(outgoing, ("seq", "head"), 0, 0, tiled=True)
    by_chip = incoming.reshape(devices // 2, 2, -1, E).astype(jnp.float32)

    running = jnp.cumsum(by_chip, axis=0)
    before = jnp.concatenate([jnp.zeros_like(running[:1]), running[:-1]], axis=0).astype(jnp.bfloat16)
    returned = lax.all_to_all(before.reshape(devices, -1, E), ("seq", "head"), 0, 0, tiled=True)
    own_rows = returned.reshape(heads, E // 2, E)
    other_rows = lax.ppermute(own_rows, "head", pairs)
    return gated_attention(core, queries, near, own_rows, other_rows, gate_logits, norm_gain)


def solution(mesh):
    rows = P(("seq", "head"), None)
    return jax.shard_map(
        on_device,
        mesh=mesh,
        in_specs=(rows, rows, rows, rows, P()),
        out_specs=rows,
        check_vma=False,
    )
```

```python
import jax
import jax.numpy as jnp
from jax import lax
from jax.experimental import pallas as pl
from jax.experimental.pallas import tpu as pltpu
from jax.sharding import PartitionSpec as P

E = 128
GROUP = 32


def state_kernel(core_ref, key_ref, value_ref, mine_ref, partner_ref, first_ref):
    first = core_ref[0] == 0
    half = E // 2
    for j in range(GROUP):
        cols = slice(j * E, (j + 1) * E)
        state = lax.dot_general(
            key_ref[:, cols], value_ref[:, cols], (((0,), (0,)), ((), ())),
            preferred_element_type=jnp.float32,
        )
        upper, lower = state[:half], state[half:]
        mine_ref[j] = jnp.where(first, upper, lower)
        partner_ref[j] = jnp.where(first, lower, upper)
        first_ref[j] = upper.astype(jnp.bfloat16)


def block_states(core, key_vectors, values):
    tokens, width = key_vectors.shape
    heads = width // E
    cols = pl.BlockSpec((tokens, GROUP * E), lambda i, core: (0, i))
    halves = pl.BlockSpec((GROUP, E // 2, E), lambda i, core: (i, 0, 0))
    shape = (heads, E // 2, E)
    return pl.pallas_call(
        state_kernel,
        grid_spec=pltpu.PrefetchScalarGridSpec(
            num_scalar_prefetch=1, grid=(heads // GROUP,), in_specs=[cols, cols], out_specs=[halves] * 3
        ),
        out_shape=[jax.ShapeDtypeStruct(shape, jnp.float32), jax.ShapeDtypeStruct(shape, jnp.float32),
                   jax.ShapeDtypeStruct(shape, jnp.bfloat16)],
    )(core.reshape(1), key_vectors, values)


def near_kernel(core_ref, query_ref, key_ref, value_ref, first_ref, partner_ref, mine_ref, near_ref, chip_ref):
    tokens = query_ref.shape[0]
    first = core_ref[0] == 0
    lower_mask = lax.broadcasted_iota(jnp.int32, (tokens, tokens), 0) >= lax.broadcasted_iota(
        jnp.int32, (tokens, tokens), 1
    )
    for j in range(GROUP):
        cols = slice(j * E, (j + 1) * E)
        query = query_ref[:, cols]
        scores = lax.dot_general(
            query, key_ref[:, cols], (((1,), (1,)), ((), ())), preferred_element_type=jnp.float32
        )
        weights = jnp.where(lower_mask, scores, 0.0).astype(jnp.bfloat16)
        total = jnp.dot(weights, value_ref[:, cols], preferred_element_type=jnp.float32)
        before = jnp.concatenate([first_ref[j], partner_ref[j].astype(jnp.bfloat16)], axis=0)
        before_part = jnp.dot(query, before, preferred_element_type=jnp.float32)
        near_ref[:, cols] = total + jnp.where(first, 0.0, before_part)
        chip_ref[j] = (mine_ref[j] + partner_ref[j]).astype(jnp.bfloat16)


def near_attention(core, queries, key_vectors, values, first_half, partner_half, mine):
    tokens, width = queries.shape
    heads = width // E
    cols = pl.BlockSpec((tokens, GROUP * E), lambda i, core: (0, i))
    halves = pl.BlockSpec((GROUP, E // 2, E), lambda i, core: (i, 0, 0))
    return pl.pallas_call(
        near_kernel,
        grid_spec=pltpu.PrefetchScalarGridSpec(
            num_scalar_prefetch=1, grid=(heads // GROUP,), in_specs=[cols, cols, cols, halves, halves, halves],
            out_specs=[cols, halves],
        ),
        out_shape=[jax.ShapeDtypeStruct((tokens, width), jnp.float32),
                   jax.ShapeDtypeStruct((heads, E // 2, E), jnp.bfloat16)],
    )(core.reshape(1), queries, key_vectors, values, first_half, partner_half, mine)


def output_kernel(core_ref, query_ref, near_ref, own_ref, other_ref, gate_ref, gain_ref,
                  out_ref, attended_ref, square_ref, opening_ref):
    step = pl.program_id(0)
    first = core_ref[0] == 0

    @pl.when(step == 0)
    def _():
        square_ref[...] = jnp.zeros_like(square_ref)

    for j in range(GROUP):
        cols = slice(j * E, (j + 1) * E)
        own = own_ref[j]
        other = other_ref[j]
        prefix = jnp.concatenate([jnp.where(first, own, other), jnp.where(first, other, own)], axis=0)
        total = near_ref[:, cols] + jnp.dot(query_ref[:, cols], prefix, preferred_element_type=jnp.float32)
        attended = total.astype(jnp.bfloat16)
        start = pl.multiple_of((step * GROUP + j) * E, E)
        attended_ref[:, pl.ds(start, E)] = attended
        features = attended.astype(jnp.float32)
        square_ref[...] += features * features
        gate = gate_ref[:, cols].astype(jnp.float32)
        opening_ref[:, pl.ds(start, E)] = 1.0 / (1.0 + jnp.exp(-gate))

    @pl.when(step == pl.num_programs(0) - 1)
    def _():
        width = attended_ref.shape[1]
        mean_square = jnp.sum(square_ref[...], axis=1, keepdims=True) / width
        scale = lax.rsqrt(mean_square + 1e-06)

        def chunk(c, carry):
            start = pl.multiple_of(c * E, E)
            window = pl.ds(start, E)
            features = attended_ref[:, window].astype(jnp.float32)
            gain = gain_ref[:, window].astype(jnp.float32)
            scaled = features * scale * gain
            scaled = scaled * opening_ref[:, window]
            out_ref[:, window] = scaled.astype(out_ref.dtype)
            return carry

        lax.fori_loop(0, width // E, chunk, 0)


def gated_attention(core, queries, near, own, other, gate_logits, norm_gain):
    tokens, width = queries.shape
    heads = width // E
    cols = pl.BlockSpec((tokens, GROUP * E), lambda i, core: (0, i))
    halves = pl.BlockSpec((GROUP, E // 2, E), lambda i, core: (i, 0, 0))
    whole = pl.BlockSpec((tokens, width), lambda i, core: (0, 0))
    return pl.pallas_call(
        output_kernel,
        grid_spec=pltpu.PrefetchScalarGridSpec(
            num_scalar_prefetch=1,
            grid=(heads // GROUP,),
            in_specs=[cols, cols, halves, halves, cols,
                      pl.BlockSpec((1, width), lambda i, core: (0, 0))],
            out_specs=whole,
            scratch_shapes=[pltpu.VMEM((tokens, width), jnp.bfloat16), pltpu.VMEM((tokens, E), jnp.float32),
                            pltpu.VMEM((tokens, width), jnp.float32)],
        ),
        out_shape=jax.ShapeDtypeStruct((tokens, width), jnp.bfloat16),
    )(core.reshape(1), queries, near, own, other, gate_logits,
      norm_gain.reshape(1, width))


def on_device(queries, key_vectors, values, gate_logits, norm_gain):
    heads = queries.shape[1] // E
    chips = lax.axis_size("head") // 2
    core = lax.axis_index("head") % 2
    pairs = [(h, h ^ 1) for h in range(2 * chips)]

    mine, for_partner, first_rows = block_states(core, key_vectors, values)
    partner_half = lax.ppermute(for_partner, "head", pairs)
    first_half = lax.ppermute(first_rows, "head", pairs)
    near, my_rows = near_attention(core, queries, key_vectors, values, first_half, partner_half, mine)
    devices = lax.axis_size("seq") * 2 * chips
    outgoing = my_rows.reshape(devices, -1, E)
    incoming = lax.all_to_all(outgoing, ("seq", "head"), 0, 0, tiled=True)
    by_chip = incoming.reshape(devices // 2, 2, -1, E).astype(jnp.float32)

    running = jnp.cumsum(by_chip, axis=0)
    before = jnp.concatenate([jnp.zeros_like(running[:1]), running[:-1]], axis=0).astype(jnp.bfloat16)
    returned = lax.all_to_all(before.reshape(devices, -1, E), ("seq", "head"), 0, 0, tiled=True)
    own_rows = returned.reshape(heads, E // 2, E)
    other_rows = lax.ppermute(own_rows, "head", pairs)
    return gated_attention(core, queries, near, own_rows, other_rows, gate_logits, norm_gain)


def solution(mesh):
    rows = P(("seq", "head"), None)
    return jax.shard_map(
        on_device,
        mesh=mesh,
        in_specs=(rows, rows, rows, rows, P()),
        out_specs=rows,
        check_vma=False,
    )
```

```python
import jax
import jax.numpy as jnp
from jax import lax
from jax.experimental import pallas as pl
from jax.experimental.pallas import tpu as pltpu
from jax.sharding import PartitionSpec as P

E = 128
GROUP = 32


def state_kernel(core_ref, key_ref, value_ref, mine_ref, partner_ref, first_ref):
    first = core_ref[0] == 0
    half = E // 2
    for j in range(GROUP):
        cols = slice(j * E, (j + 1) * E)
        state = lax.dot_general(
            key_ref[:, cols], value_ref[:, cols], (((0,), (0,)), ((), ())),
            preferred_element_type=jnp.float32,
        )
        upper, lower = state[:half], state[half:]
        mine_ref[j] = jnp.where(first, upper, lower)
        partner_ref[j] = jnp.where(first, lower, upper)
        first_ref[j] = upper.astype(jnp.bfloat16)


def block_states(core, key_vectors, values):
    tokens, width = key_vectors.shape
    heads = width // E
    cols = pl.BlockSpec((tokens, GROUP * E), lambda i, core: (0, i))
    halves = pl.BlockSpec((GROUP, E // 2, E), lambda i, core: (i, 0, 0))
    shape = (heads, E // 2, E)
    return pl.pallas_call(
        state_kernel,
        grid_spec=pltpu.PrefetchScalarGridSpec(
            num_scalar_prefetch=1, grid=(heads // GROUP,), in_specs=[cols, cols], out_specs=[halves] * 3
        ),
        out_shape=[jax.ShapeDtypeStruct(shape, jnp.float32), jax.ShapeDtypeStruct(shape, jnp.float32),
                   jax.ShapeDtypeStruct(shape, jnp.bfloat16)],
    )(core.reshape(1), key_vectors, values)


def near_kernel(core_ref, query_ref, key_ref, value_ref, first_ref, partner_ref, mine_ref, near_ref, chip_ref):
    tokens = query_ref.shape[0]
    first = core_ref[0] == 0
    lower_mask = lax.broadcasted_iota(jnp.int32, (tokens, tokens), 0) >= lax.broadcasted_iota(
        jnp.int32, (tokens, tokens), 1
    )
    for j in range(GROUP):
        cols = slice(j * E, (j + 1) * E)
        query = query_ref[:, cols]
        scores = lax.dot_general(
            query, key_ref[:, cols], (((1,), (1,)), ((), ())), preferred_element_type=jnp.float32
        )
        weights = jnp.where(lower_mask, scores, 0.0).astype(jnp.bfloat16)
        total = jnp.dot(weights, value_ref[:, cols], preferred_element_type=jnp.float32)
        before = jnp.concatenate([first_ref[j], partner_ref[j].astype(jnp.bfloat16)], axis=0)
        before_part = jnp.dot(query, before, preferred_element_type=jnp.float32)
        near_ref[:, cols] = total + jnp.where(first, 0.0, before_part)
        chip_ref[j] = (mine_ref[j] + partner_ref[j]).astype(jnp.bfloat16)


def near_attention(core, queries, key_vectors, values, first_half, partner_half, mine):
    tokens, width = queries.shape
    heads = width // E
    cols = pl.BlockSpec((tokens, GROUP * E), lambda i, core: (0, i))
    halves = pl.BlockSpec((GROUP, E // 2, E), lambda i, core: (i, 0, 0))
    return pl.pallas_call(
        near_kernel,
        grid_spec=pltpu.PrefetchScalarGridSpec(
            num_scalar_prefetch=1, grid=(heads // GROUP,), in_specs=[cols, cols, cols, halves, halves, halves],
            out_specs=[cols, halves],
        ),
        out_shape=[jax.ShapeDtypeStruct((tokens, width), jnp.float32),
                   jax.ShapeDtypeStruct((heads, E // 2, E), jnp.bfloat16)],
    )(core.reshape(1), queries, key_vectors, values, first_half, partner_half, mine)


def output_kernel(core_ref, query_ref, near_ref, own_ref, other_ref, gate_ref, gain_ref,
                  out_ref, attended_ref, square_ref, opening_ref):
    step = pl.program_id(0)
    first = core_ref[0] == 0

    @pl.when(step == 0)
    def _():
        square_ref[...] = jnp.zeros_like(square_ref)

    for j in range(GROUP):
        cols = slice(j * E, (j + 1) * E)
        own = own_ref[j]
        other = other_ref[j]
        prefix = jnp.concatenate([jnp.where(first, own, other), jnp.where(first, other, own)], axis=0)
        total = near_ref[:, cols] + jnp.dot(query_ref[:, cols], prefix, preferred_element_type=jnp.float32)
        attended = total.astype(jnp.bfloat16)
        start = pl.multiple_of((step * GROUP + j) * E, E)
        attended_ref[:, pl.ds(start, E)] = attended
        features = attended.astype(jnp.float32)
        square_ref[...] += features * features
        gate = gate_ref[:, cols].astype(jnp.float32)
        gain = gain_ref[:, pl.ds(start, E)].astype(jnp.float32)
        opening_ref[:, pl.ds(start, E)] = gain * (0.5 + 0.5 * jnp.tanh(0.5 * gate))

    @pl.when(step == pl.num_programs(0) - 1)
    def _():
        width = attended_ref.shape[1]
        mean_square = jnp.sum(square_ref[...], axis=1, keepdims=True) / width
        scale = lax.rsqrt(mean_square + 1e-06)

        def chunk(c, carry):
            start = pl.multiple_of(c * E, E)
            window = pl.ds(start, E)
            features = attended_ref[:, window].astype(jnp.float32)
            scaled = features * scale * opening_ref[:, window]
            out_ref[:, window] = scaled.astype(out_ref.dtype)
            return carry

        lax.fori_loop(0, width // E, chunk, 0)


def gated_attention(core, queries, near, own, other, gate_logits, norm_gain):
    tokens, width = queries.shape
    heads = width // E
    cols = pl.BlockSpec((tokens, GROUP * E), lambda i, core: (0, i))
    halves = pl.BlockSpec((GROUP, E // 2, E), lambda i, core: (i, 0, 0))
    whole = pl.BlockSpec((tokens, width), lambda i, core: (0, 0))
    return pl.pallas_call(
        output_kernel,
        grid_spec=pltpu.PrefetchScalarGridSpec(
            num_scalar_prefetch=1,
            grid=(heads // GROUP,),
            in_specs=[cols, cols, halves, halves, cols,
                      pl.BlockSpec((1, width), lambda i, core: (0, 0))],
            out_specs=whole,
            scratch_shapes=[pltpu.VMEM((tokens, width), jnp.bfloat16), pltpu.VMEM((tokens, E), jnp.float32),
                            pltpu.VMEM((tokens, width), jnp.float32)],
        ),
        out_shape=jax.ShapeDtypeStruct((tokens, width), jnp.bfloat16),
    )(core.reshape(1), queries, near, own, other, gate_logits,
      norm_gain.reshape(1, width))


def on_device(queries, key_vectors, values, gate_logits, norm_gain):
    heads = queries.shape[1] // E
    chips = lax.axis_size("head") // 2
    core = lax.axis_index("head") % 2
    pairs = [(h, h ^ 1) for h in range(2 * chips)]

    mine, for_partner, first_rows = block_states(core, key_vectors, values)
    partner_half = lax.ppermute(for_partner, "head", pairs)
    first_half = lax.ppermute(first_rows, "head", [(h, h + 1) for h in range(0, 2 * chips, 2)])
    near, my_rows = near_attention(core, queries, key_vectors, values, first_half, partner_half, mine)
    devices = lax.axis_size("seq") * 2 * chips
    outgoing = my_rows.reshape(devices, -1, E)
    incoming = lax.all_to_all(outgoing, ("seq", "head"), 0, 0, tiled=True)
    by_chip = incoming.reshape(devices // 2, 2, -1, E).astype(jnp.float32)

    running = jnp.cumsum(by_chip, axis=0)
    before = jnp.concatenate([jnp.zeros_like(running[:1]), running[:-1]], axis=0).astype(jnp.bfloat16)
    returned = lax.all_to_all(before.reshape(devices, -1, E), ("seq", "head"), 0, 0, tiled=True)
    own_rows = returned.reshape(heads, E // 2, E)
    other_rows = lax.ppermute(own_rows, "head", pairs)
    return gated_attention(core, queries, near, own_rows, other_rows, gate_logits, norm_gain)


def solution(mesh):
    rows = P(("seq", "head"), None)
    return jax.shard_map(
        on_device,
        mesh=mesh,
        in_specs=(rows, rows, rows, rows, P()),
        out_specs=rows,
        check_vma=False,
    )
```

```python
import jax
import jax.numpy as jnp
from jax import lax
from jax.experimental import pallas as pl
from jax.experimental.pallas import tpu as pltpu
from jax.sharding import Mesh
from jax.sharding import PartitionSpec as P

E = 128
GROUP = 32


def state_kernel(core_ref, key_ref, value_ref, mine_ref, partner_ref, first_ref):
    first = core_ref[0] == 0
    half = E // 2
    for j in range(GROUP):
        cols = slice(j * E, (j + 1) * E)
        state = lax.dot_general(
            key_ref[:, cols], value_ref[:, cols], (((0,), (0,)), ((), ())),
            preferred_element_type=jnp.float32,
        )
        upper, lower = state[:half], state[half:]
        mine_ref[j] = jnp.where(first, upper, lower)
        partner_ref[j] = jnp.where(first, lower, upper)
        first_ref[j] = upper.astype(jnp.bfloat16)


def block_states(core, key_vectors, values):
    tokens, width = key_vectors.shape
    heads = width // E
    cols = pl.BlockSpec((tokens, GROUP * E), lambda i, core: (0, i))
    halves = pl.BlockSpec((GROUP, E // 2, E), lambda i, core: (i, 0, 0))
    shape = (heads, E // 2, E)
    return pl.pallas_call(
        state_kernel,
        grid_spec=pltpu.PrefetchScalarGridSpec(
            num_scalar_prefetch=1, grid=(heads // GROUP,), in_specs=[cols, cols], out_specs=[halves] * 3
        ),
        out_shape=[jax.ShapeDtypeStruct(shape, jnp.float32), jax.ShapeDtypeStruct(shape, jnp.float32),
                   jax.ShapeDtypeStruct(shape, jnp.bfloat16)],
    )(core.reshape(1), key_vectors, values)


def near_kernel(core_ref, query_ref, key_ref, value_ref, first_ref, partner_ref, mine_ref, near_ref, chip_ref):
    tokens = query_ref.shape[0]
    first = core_ref[0] == 0
    lower_mask = lax.broadcasted_iota(jnp.int32, (tokens, tokens), 0) >= lax.broadcasted_iota(
        jnp.int32, (tokens, tokens), 1
    )
    for j in range(GROUP):
        cols = slice(j * E, (j + 1) * E)
        query = query_ref[:, cols]
        scores = lax.dot_general(
            query, key_ref[:, cols], (((1,), (1,)), ((), ())), preferred_element_type=jnp.float32
        )
        weights = jnp.where(lower_mask, scores, 0.0).astype(jnp.bfloat16)
        total = jnp.dot(weights, value_ref[:, cols], preferred_element_type=jnp.float32)
        before = jnp.concatenate([first_ref[j], partner_ref[j].astype(jnp.bfloat16)], axis=0)
        before_part = jnp.dot(query, before, preferred_element_type=jnp.float32)
        near_ref[:, cols] = total + jnp.where(first, 0.0, before_part)
        chip_ref[j] = (mine_ref[j] + partner_ref[j]).astype(jnp.bfloat16)


def near_attention(core, queries, key_vectors, values, first_half, partner_half, mine):
    tokens, width = queries.shape
    heads = width // E
    cols = pl.BlockSpec((tokens, GROUP * E), lambda i, core: (0, i))
    halves = pl.BlockSpec((GROUP, E // 2, E), lambda i, core: (i, 0, 0))
    return pl.pallas_call(
        near_kernel,
        grid_spec=pltpu.PrefetchScalarGridSpec(
            num_scalar_prefetch=1, grid=(heads // GROUP,), in_specs=[cols, cols, cols, halves, halves, halves],
            out_specs=[cols, halves],
        ),
        out_shape=[jax.ShapeDtypeStruct((tokens, width), jnp.float32),
                   jax.ShapeDtypeStruct((heads, E // 2, E), jnp.bfloat16)],
    )(core.reshape(1), queries, key_vectors, values, first_half, partner_half, mine)


def output_kernel(core_ref, query_ref, near_ref, own_ref, other_ref, gate_ref, gain_ref,
                  out_ref, attended_ref, square_ref, opening_ref):
    step = pl.program_id(0)
    first = core_ref[0] == 0

    @pl.when(step == 0)
    def _():
        square_ref[...] = jnp.zeros_like(square_ref)

    for j in range(GROUP):
        cols = slice(j * E, (j + 1) * E)
        own = own_ref[j]
        other = other_ref[j]
        prefix = jnp.concatenate([jnp.where(first, own, other), jnp.where(first, other, own)], axis=0)
        total = near_ref[:, cols] + jnp.dot(query_ref[:, cols], prefix, preferred_element_type=jnp.float32)
        attended = total.astype(jnp.bfloat16)
        start = pl.multiple_of((step * GROUP + j) * E, E)
        attended_ref[:, pl.ds(start, E)] = attended
        features = attended.astype(jnp.float32)
        square_ref[...] += features * features
        gate = gate_ref[:, cols].astype(jnp.float32)
        gain = gain_ref[:, pl.ds(start, E)].astype(jnp.float32)
        opening_ref[:, pl.ds(start, E)] = gain * (0.5 + 0.5 * jnp.tanh(0.5 * gate))

    @pl.when(step == pl.num_programs(0) - 1)
    def _():
        width = attended_ref.shape[1]
        mean_square = jnp.sum(square_ref[...], axis=1, keepdims=True) / width
        scale = lax.rsqrt(mean_square + 1e-06)

        def chunk(c, carry):
            start = pl.multiple_of(c * E, E)
            window = pl.ds(start, E)
            features = attended_ref[:, window].astype(jnp.float32)
            scaled = features * scale * opening_ref[:, window]
            out_ref[:, window] = scaled.astype(out_ref.dtype)
            return carry

        lax.fori_loop(0, width // E, chunk, 0)


def gated_attention(core, queries, near, own, other, gate_logits, norm_gain):
    tokens, width = queries.shape
    heads = width // E
    cols = pl.BlockSpec((tokens, GROUP * E), lambda i, core: (0, i))
    halves = pl.BlockSpec((GROUP, E // 2, E), lambda i, core: (i, 0, 0))
    whole = pl.BlockSpec((tokens, width), lambda i, core: (0, 0))
    return pl.pallas_call(
        output_kernel,
        grid_spec=pltpu.PrefetchScalarGridSpec(
            num_scalar_prefetch=1,
            grid=(heads // GROUP,),
            in_specs=[cols, cols, halves, halves, cols,
                      pl.BlockSpec((1, width), lambda i, core: (0, 0))],
            out_specs=whole,
            scratch_shapes=[pltpu.VMEM((tokens, width), jnp.bfloat16), pltpu.VMEM((tokens, E), jnp.float32),
                            pltpu.VMEM((tokens, width), jnp.float32)],
        ),
        out_shape=jax.ShapeDtypeStruct((tokens, width), jnp.bfloat16),
    )(core.reshape(1), queries, near, own, other, gate_logits,
      norm_gain.reshape(1, width))


def on_device(queries, key_vectors, values, gate_logits, norm_gain):
    heads = queries.shape[1] // E
    chips = lax.axis_size("z")
    core = lax.axis_index("core")
    pairs = [(0, 1), (1, 0)]

    mine, for_partner, first_rows = block_states(core, key_vectors, values)
    partner_half = lax.ppermute(for_partner, "core", pairs)
    first_half = lax.ppermute(first_rows, "core", [(0, 1)])
    near, my_rows = near_attention(core, queries, key_vectors, values, first_half, partner_half, mine)
    owners = lax.axis_size("seq") * chips
    outgoing = my_rows.reshape(owners, -1, E)
    by_chip = lax.all_to_all(outgoing, ("seq", "z"), 0, 0, tiled=True).astype(jnp.float32)

    running = jnp.cumsum(by_chip, axis=0)
    before = jnp.concatenate([jnp.zeros_like(running[:1]), running[:-1]], axis=0).astype(jnp.bfloat16)
    returned = lax.all_to_all(before, ("seq", "z"), 0, 0, tiled=True)
    own_rows = returned.reshape(heads, E // 2, E)
    other_rows = lax.ppermute(own_rows, "core", pairs)
    return gated_attention(core, queries, near, own_rows, other_rows, gate_logits, norm_gain)


def solution(mesh):
    seq = mesh.shape["seq"]
    cores = 2
    split = Mesh(mesh.devices.reshape(seq, mesh.shape["head"] // cores, cores), ("seq", "z", "core"))
    rows = P(("seq", "z", "core"), None)
    return jax.shard_map(
        on_device,
        mesh=split,
        in_specs=(rows, rows, rows, rows, P()),
        out_specs=rows,
        check_vma=False,
    )
```

```python
import jax
import jax.numpy as jnp
from jax import lax
from jax.experimental import pallas as pl
from jax.experimental.pallas import tpu as pltpu
from jax.sharding import PartitionSpec as P

E = 128
GROUP = 32


def state_kernel(core_ref, key_ref, value_ref, mine_ref, whole_ref):
    first = core_ref[0] == 0
    half = E // 2
    for j in range(GROUP):
        cols = slice(j * E, (j + 1) * E)
        state = lax.dot_general(
            key_ref[:, cols], value_ref[:, cols], (((0,), (0,)), ((), ())),
            preferred_element_type=jnp.float32,
        )
        mine_ref[j] = jnp.where(first, state[:half], state[half:])
        whole_ref[j] = state.astype(jnp.bfloat16)


def block_states(core, key_vectors, values):
    tokens, width = key_vectors.shape
    heads = width // E
    cols = pl.BlockSpec((tokens, GROUP * E), lambda i, core: (0, i))
    halves = pl.BlockSpec((GROUP, E // 2, E), lambda i, core: (i, 0, 0))
    wholes = pl.BlockSpec((GROUP, E, E), lambda i, core: (i, 0, 0))
    return pl.pallas_call(
        state_kernel,
        grid_spec=pltpu.PrefetchScalarGridSpec(
            num_scalar_prefetch=1, grid=(heads // GROUP,), in_specs=[cols, cols], out_specs=[halves, wholes]
        ),
        out_shape=[jax.ShapeDtypeStruct((heads, E // 2, E), jnp.float32),
                   jax.ShapeDtypeStruct((heads, E, E), jnp.bfloat16)],
    )(core.reshape(1), key_vectors, values)


def near_kernel(core_ref, query_ref, key_ref, value_ref, partner_ref, mine_ref, near_ref, chip_ref):
    tokens = query_ref.shape[0]
    first = core_ref[0] == 0
    half = E // 2
    lower_mask = lax.broadcasted_iota(jnp.int32, (tokens, tokens), 0) >= lax.broadcasted_iota(
        jnp.int32, (tokens, tokens), 1
    )
    for j in range(GROUP):
        cols = slice(j * E, (j + 1) * E)
        query = query_ref[:, cols]
        scores = lax.dot_general(
            query, key_ref[:, cols], (((1,), (1,)), ((), ())), preferred_element_type=jnp.float32
        )
        weights = jnp.where(lower_mask, scores, 0.0).astype(jnp.bfloat16)
        total = jnp.dot(weights, value_ref[:, cols], preferred_element_type=jnp.float32)
        partner = partner_ref[j]
        before_part = jnp.dot(query, partner, preferred_element_type=jnp.float32)
        near_ref[:, cols] = total + jnp.where(first, 0.0, before_part)
        partner_rows = jnp.where(first, partner[:half], partner[half:]).astype(jnp.float32)
        chip_ref[j] = (mine_ref[j] + partner_rows).astype(jnp.bfloat16)


def near_attention(core, queries, key_vectors, values, partner_state, mine):
    tokens, width = queries.shape
    heads = width // E
    cols = pl.BlockSpec((tokens, GROUP * E), lambda i, core: (0, i))
    halves = pl.BlockSpec((GROUP, E // 2, E), lambda i, core: (i, 0, 0))
    wholes = pl.BlockSpec((GROUP, E, E), lambda i, core: (i, 0, 0))
    return pl.pallas_call(
        near_kernel,
        grid_spec=pltpu.PrefetchScalarGridSpec(
            num_scalar_prefetch=1, grid=(heads // GROUP,), in_specs=[cols, cols, cols, wholes, halves],
            out_specs=[cols, halves],
        ),
        out_shape=[jax.ShapeDtypeStruct((tokens, width), jnp.float32),
                   jax.ShapeDtypeStruct((heads, E // 2, E), jnp.bfloat16)],
    )(core.reshape(1), queries, key_vectors, values, partner_state, mine)


def output_kernel(core_ref, query_ref, near_ref, own_ref, other_ref, gate_ref, gain_ref,
                  out_ref, attended_ref, square_ref, opening_ref):
    step = pl.program_id(0)
    first = core_ref[0] == 0

    @pl.when(step == 0)
    def _():
        square_ref[...] = jnp.zeros_like(square_ref)

    for j in range(GROUP):
        cols = slice(j * E, (j + 1) * E)
        own = own_ref[j]
        other = other_ref[j]
        prefix = jnp.concatenate([jnp.where(first, own, other), jnp.where(first, other, own)], axis=0)
        total = near_ref[:, cols] + jnp.dot(query_ref[:, cols], prefix, preferred_element_type=jnp.float32)
        attended = total.astype(jnp.bfloat16)
        start = pl.multiple_of((step * GROUP + j) * E, E)
        attended_ref[:, pl.ds(start, E)] = attended
        features = attended.astype(jnp.float32)
        square_ref[...] += features * features
        gate = gate_ref[:, cols].astype(jnp.float32)
        gain = gain_ref[:, pl.ds(start, E)].astype(jnp.float32)
        opening_ref[:, pl.ds(start, E)] = gain * (0.5 + 0.5 * jnp.tanh(0.5 * gate))

    @pl.when(step == pl.num_programs(0) - 1)
    def _():
        width = attended_ref.shape[1]
        mean_square = jnp.sum(square_ref[...], axis=1, keepdims=True) / width
        scale = lax.rsqrt(mean_square + 1e-06)

        def chunk(c, carry):
            start = pl.multiple_of(c * E, E)
            window = pl.ds(start, E)
            features = attended_ref[:, window].astype(jnp.float32)
            scaled = features * scale * opening_ref[:, window]
            out_ref[:, window] = scaled.astype(out_ref.dtype)
            return carry

        lax.fori_loop(0, width // E, chunk, 0)


def gated_attention(core, queries, near, own, other, gate_logits, norm_gain):
    tokens, width = queries.shape
    heads = width // E
    cols = pl.BlockSpec((tokens, GROUP * E), lambda i, core: (0, i))
    halves = pl.BlockSpec((GROUP, E // 2, E), lambda i, core: (i, 0, 0))
    whole = pl.BlockSpec((tokens, width), lambda i, core: (0, 0))
    return pl.pallas_call(
        output_kernel,
        grid_spec=pltpu.PrefetchScalarGridSpec(
            num_scalar_prefetch=1,
            grid=(heads // GROUP,),
            in_specs=[cols, cols, halves, halves, cols,
                      pl.BlockSpec((1, width), lambda i, core: (0, 0))],
            out_specs=whole,
            scratch_shapes=[pltpu.VMEM((tokens, width), jnp.bfloat16), pltpu.VMEM((tokens, E), jnp.float32),
                            pltpu.VMEM((tokens, width), jnp.float32)],
        ),
        out_shape=jax.ShapeDtypeStruct((tokens, width), jnp.bfloat16),
    )(core.reshape(1), queries, near, own, other, gate_logits,
      norm_gain.reshape(1, width))


def on_device(queries, key_vectors, values, gate_logits, norm_gain):
    heads = queries.shape[1] // E
    chips = lax.axis_size("head") // 2
    core = lax.axis_index("head") % 2
    pairs = [(h, h ^ 1) for h in range(2 * chips)]

    mine, whole = block_states(core, key_vectors, values)
    partner_state = lax.ppermute(whole, "head", pairs)
    near, my_rows = near_attention(core, queries, key_vectors, values, partner_state, mine)
    devices = lax.axis_size("seq") * 2 * chips
    outgoing = my_rows.reshape(devices, -1, E)
    incoming = lax.all_to_all(outgoing, ("seq", "head"), 0, 0, tiled=True)
    by_chip = incoming.reshape(devices // 2, 2, -1, E).astype(jnp.float32)

    running = jnp.cumsum(by_chip, axis=0)
    before = jnp.concatenate([jnp.zeros_like(running[:1]), running[:-1]], axis=0).astype(jnp.bfloat16)
    returned = lax.all_to_all(before.reshape(devices, -1, E), ("seq", "head"), 0, 0, tiled=True)
    own_rows = returned.reshape(heads, E // 2, E)
    other_rows = lax.ppermute(own_rows, "head", pairs)
    return gated_attention(core, queries, near, own_rows, other_rows, gate_logits, norm_gain)


def solution(mesh):
    rows = P(("seq", "head"), None)
    return jax.shard_map(
        on_device,
        mesh=mesh,
        in_specs=(rows, rows, rows, rows, P()),
        out_specs=rows,
        check_vma=False,
    )
```
